32 devices in a mesh: ctx: 8 (over y, x, core), mp: 4 (over z).
Axes of the slice: x: 2, y: 2, z: 4, core: 2. Of those that a mesh axis runs over, the one named last changes fastest.
Arguments:
- cotangent: bfloat16 [1536, 8192], P('ctx', 'mp'), may hold values from -6 to 6
- out_weight: bfloat16 [8192, 8192], P('mp', 'ctx'), may hold values from -0.0625 to 0.0625
- query_act: bfloat16 [1536, 8192], P('ctx', 'mp'), may hold values from -6 to 6
- key_act: bfloat16 [1536, 8192], P('ctx', 'mp'), may hold values from -6 to 6
- value_act: bfloat16 [1536, 8192], P('ctx', 'mp'), may hold values from -6 to 6
- filters: float32 [512, 128], replicated, may hold values from -0.5 to 0.5
Outputs:
- grad_query: bfloat16 [1536, 8192], P('ctx', 'mp')
- grad_key: bfloat16 [1536, 8192], P('ctx', 'mp')
- grad_value: bfloat16 [1536, 8192], P('ctx', 'mp')
- grad_filters: float32 [512, 128], replicated
The draws below stay inside these ranges and needn't reach their ends.
All inputs are finite; a program needn't handle non-finite values.
Results may differ from the reference program's by a relative error of at most 0.0051.
Values may be sent and summed in bfloat16 or wider, within the bound.
No kernel may reach another device: no remote copies, remote signals or barrier semaphores. Data moves between devices by JAX's collectives and lax.ppermute only.
A program may use at most 128 MiB of HBM per device.

```python
import jax
import jax.numpy as jnp
from jax import lax

D = 8192
G = 512
FL = 128
TOKENS = 1536


def block_scale(own_key, extent, shards, low, top_value):
    def one(axis_at, shards_of):
        heights = jax.random.uniform(jax.random.fold_in(jax.random.fold_in(own_key, 6), axis_at), (shards_of,), jnp.float32, low / len(shards), top_value / len(shards))
        return jnp.repeat(jnp.exp(heights), extent[axis_at] // shards_of).reshape((-1,) + (1,) * (len(extent) - axis_at - 1))

    loudness = one(*shards[0])
    for cut in shards[1:]:
        loudness = loudness * one(*cut)
    return loudness


def noise(key, shape, scale, reach, split=(), held_as=jnp.bfloat16):
    level = block_scale(key, shape, split, -0.22, 0.18) if split else 1.0
    result = jax.random.normal(key, shape, jnp.float32) * scale * level
    return jnp.minimum(jnp.maximum(result, -reach), reach).astype(held_as)


def setup_inputs(seed: int = 0) -> dict:
    seeds = jax.random.split(jax.random.key(seed), 7)
    cotangent = noise(seeds[0], (TOKENS, D), 1.0, 6.0, ((0, 8), (1, 4)))
    out_weight = noise(seeds[1], (D, D), D ** -0.5, 0.0625, ((0, 4), (1, 8)))
    query_act = noise(seeds[2], (TOKENS, D), 1.0, 6.0, ((0, 8), (1, 4)))
    key_act = noise(seeds[3], (TOKENS, D), 1.0, 6.0, ((0, 8), (1, 4)))
    value_act = noise(seeds[4], (TOKENS, D), 1.0, 6.0, ((0, 8), (1, 4)))
    filters = noise(seeds[5], (G, FL), FL ** -0.5, 0.5, (), jnp.float32)
    return {"cotangent": cotangent, "out_weight": out_weight, "query_act": query_act, "key_act": key_act, "value_act": value_act, "filters": filters}


def causal(widened, taps, rows, prev):
    def step(shift, total):
        window = lax.dynamic_slice_in_dim(widened, (prev - shift).astype(jnp.int32), rows, 0)
        weight = lax.dynamic_slice_in_dim(taps, shift.astype(jnp.int32), 1, 0)
        return total + weight * window
    return lax.fori_loop(jnp.int32(0), jnp.int32(prev + 1), step, jnp.zeros((rows, widened.shape[1]), widened.dtype))


def anticausal(trailing, taps, rows, prev):
    def step(shift, total):
        window = lax.dynamic_slice_in_dim(trailing, shift.astype(jnp.int32), rows, 0)
        weight = lax.dynamic_slice_in_dim(taps, shift.astype(jnp.int32), 1, 0)
        return total + weight * window
    return lax.fori_loop(jnp.int32(0), jnp.int32(prev + 1), step, jnp.zeros((rows, trailing.shape[1]), trailing.dtype))


def lagged(widened, gradient, prev):
    rows = gradient.shape[0]

    def one_lag(shift):
        window = lax.dynamic_slice_in_dim(widened, (prev - shift).astype(jnp.int32), rows, 0)
        return jnp.sum(window * gradient, axis=0)
    return lax.map(one_lag, jnp.arange(prev + 1, dtype=jnp.int32))


def reference(cotangent, out_weight, query_act, key_act, value_act, filters):
    prev = FL - 1
    product = (key_act.astype(jnp.float32) * value_act.astype(jnp.float32)).astype(jnp.bfloat16)
    onehot = (jnp.arange(D)[None, :] // (D // G) == jnp.arange(G)[:, None]).astype(jnp.float32)
    taps = jnp.dot(filters.T, onehot, precision=lax.Precision.HIGHEST)
    widened = jnp.concatenate([jnp.zeros((prev, D), jnp.float32), product.astype(jnp.float32)], 0)
    mixed = causal(widened, taps, TOKENS, prev)
    grad_mixed = jnp.dot(cotangent, out_weight.T, preferred_element_type=jnp.float32)
    grad_query = (grad_mixed * mixed).astype(jnp.bfloat16)
    grad_conv = (grad_mixed * query_act.astype(jnp.float32)).astype(jnp.bfloat16)
    conv_wide = grad_conv.astype(jnp.float32)
    trailing = jnp.concatenate([conv_wide, jnp.zeros((prev, D), jnp.float32)], 0)
    grad_product = anticausal(trailing, taps, TOKENS, prev)
    grad_key = (grad_product * value_act.astype(jnp.float32)).astype(jnp.bfloat16)
    grad_value = (grad_product * key_act.astype(jnp.float32)).astype(jnp.bfloat16)
    corr = lagged(widened, conv_wide, prev)
    scale = (TOKENS * D / G) ** -0.5
    grad_filters = jnp.dot(onehot, corr.T, precision=lax.Precision.HIGHEST) * scale
    return grad_query, grad_key, grad_value, grad_filters
```

```python
import jax
import jax.numpy as jnp
from jax import lax
from jax.sharding import PartitionSpec as P


def contract(left, right):
    return lax.dot_general(
        left, right, (((1,), (1,)), ((), ())), preferred_element_type=jnp.float32
    )


def toeplitz(seq, block, width):
    groups = seq.shape[0]
    flat = jnp.tile(seq, (1, block))[:, : block * width]
    return flat.reshape(groups, block, width)


def split_bf16(x):
    hi = x.astype(jnp.bfloat16)
    lo = (x - hi.astype(jnp.float32)).astype(jnp.bfloat16)
    return hi, lo


def windows(x, tiles, block, width):
    return jnp.stack([x[k * block : k * block + width] for k in range(tiles)])


def filter_apply(mats, wins, groups, per_group):
    tiles, width, chans = wins.shape
    w4 = wins.reshape(tiles, width, groups, per_group)
    total = None
    for m in mats:
        part = jnp.einsum("gij,kjgc->kigc", m, w4, preferred_element_type=jnp.float32)
        total = part if total is None else total + part
    block = mats[0].shape[1]
    return total.reshape(tiles * block, chans)


def body(cotangent, out_weight, query_act, key_act, value_act, filters):
    rows, chans = cotangent.shape
    groups, flen = filters.shape
    ctx_count = lax.axis_size("ctx")
    mp_count = lax.axis_size("mp")
    per_group = chans * mp_count // groups
    local_groups = chans // per_group
    halo = flen
    block = 64 if rows % 64 == 0 else rows
    tiles = rows // block
    width = block + halo

    panel = lax.all_gather(out_weight, "ctx", axis=1, tiled=True)
    grad_mixed = contract(lax.all_gather(cotangent, "mp", axis=1, tiled=True), panel)
    product = (key_act.astype(jnp.float32) * value_act.astype(jnp.float32)).astype(jnp.bfloat16)
    grad_conv = (grad_mixed * query_act.astype(jnp.float32)).astype(jnp.bfloat16)

    fwd = [(k, k + 1) for k in range(ctx_count - 1)]
    bwd = [(k + 1, k) for k in range(ctx_count - 1)]
    prev_tail = lax.ppermute(product[rows - halo :], "ctx", fwd)
    next_head = lax.ppermute(grad_conv[:halo], "ctx", bwd)

    taps = lax.dynamic_slice_in_dim(filters, lax.axis_index("mp") * local_groups, local_groups, 0)
    pad = jnp.zeros((local_groups, width + 1 - flen - 1), jnp.float32)
    one = jnp.zeros((local_groups, 1), jnp.float32)
    seq_causal = jnp.concatenate([one, taps[:, ::-1], pad], 1)
    seq_anti = jnp.concatenate([taps, pad, one], 1)
    mats_causal = split_bf16(toeplitz(seq_causal, block, width))
    mats_anti = split_bf16(toeplitz(seq_anti, block, width))

    widened = jnp.concatenate([prev_tail, product], 0)
    trailing = jnp.concatenate([grad_conv, next_head], 0)
    win_prod = windows(widened, tiles, block, width)
    win_grad = windows(trailing, tiles, block, width)

    mixed = filter_apply(mats_causal, win_prod, local_groups, per_group)
    grad_product = filter_apply(mats_anti, win_grad, local_groups, per_group)

    gc4 = grad_conv.reshape(tiles, block, local_groups, per_group)
    wp4 = win_prod.reshape(tiles, width, local_groups, per_group)
    cross = jnp.einsum("kigc,kjgc->gij", gc4, wp4, preferred_element_type=jnp.float32)
    cross = jnp.pad(cross.reshape(local_groups, block * width), ((0, 0), (0, block)))
    diag = cross.reshape(local_groups, block, width + 1)[:, :, 1 : halo + 1].sum(axis=1)
    scale = (rows * ctx_count * per_group) ** (-0.5)
    local_filters = lax.psum(diag[:, ::-1], "ctx") * scale
    grad_filters = lax.all_gather(local_filters, "mp", axis=0, tiled=True)

    grad_query = (grad_mixed * mixed).astype(jnp.bfloat16)
    grad_key = (grad_product * value_act.astype(jnp.float32)).astype(jnp.bfloat16)
    grad_value = (grad_product * key_act.astype(jnp.float32)).astype(jnp.bfloat16)
    return (grad_query, grad_key, grad_value, grad_filters)


def solution(mesh):
    in_specs = (P("ctx", "mp"), P("mp", "ctx"), P("ctx", "mp"), P("ctx", "mp"), P("ctx", "mp"), P())
    out_specs = (P("ctx", "mp"), P("ctx", "mp"), P("ctx", "mp"), P())
    return jax.shard_map(body, mesh=mesh, in_specs=in_specs, out_specs=out_specs, check_vma=False)
```

```python
import jax
import jax.numpy as jnp
from jax import lax
from jax.sharding import PartitionSpec as P


def contract(left, right):
    return lax.dot_general(
        left, right, (((1,), (1,)), ((), ())), preferred_element_type=jnp.float32
    )


def toeplitz(seq, block, width):
    groups = seq.shape[0]
    flat = jnp.tile(seq, (1, block))[:, : block * width]
    return flat.reshape(groups, block, width)


def split_bf16(x):
    hi = lax.reduce_precision(x, exponent_bits=8, mantissa_bits=7)
    lo = x - hi
    return hi.astype(jnp.bfloat16), lo.astype(jnp.bfloat16)


def windows(x, tiles, block, width):
    return jnp.stack([x[k * block : k * block + width] for k in range(tiles)])


def filter_apply(mats, wins, groups, per_group):
    tiles, width, chans = wins.shape
    w4 = wins.reshape(tiles, width, groups, per_group)
    total = None
    for m in mats:
        part = jnp.einsum("gij,kjgc->kigc", m, w4, preferred_element_type=jnp.float32)
        total = part if total is None else total + part
    block = mats[0].shape[1]
    return total.reshape(tiles * block, chans)


def body(cotangent, out_weight, query_act, key_act, value_act, filters):
    rows, chans = cotangent.shape
    groups, flen = filters.shape
    ctx_count = lax.axis_size("ctx")
    mp_count = lax.axis_size("mp")
    per_group = chans * mp_count // groups
    local_groups = chans // per_group
    halo = flen
    block = 64 if rows % 64 == 0 else rows
    tiles = rows // block
    width = block + halo

    cot_rows = lax.all_gather(cotangent, "mp", axis=1, tiled=True)
    cot_cols = lax.all_to_all(cot_rows, "ctx", split_axis=1, concat_axis=0, tiled=True)
    partial = contract(cot_cols, out_weight)
    grad_mixed = lax.psum_scatter(partial, "ctx", scatter_dimension=0, tiled=True)
    product = (key_act.astype(jnp.float32) * value_act.astype(jnp.float32)).astype(jnp.bfloat16)
    grad_conv = (grad_mixed * query_act.astype(jnp.float32)).astype(jnp.bfloat16)

    fwd = [(k, k + 1) for k in range(ctx_count - 1)]
    bwd = [(k + 1, k) for k in range(ctx_count - 1)]
    prev_tail = lax.ppermute(product[rows - halo :], "ctx", fwd)
    next_head = lax.ppermute(grad_conv[:halo], "ctx", bwd)

    taps = lax.dynamic_slice_in_dim(filters, lax.axis_index("mp") * local_groups, local_groups, 0)
    pad = jnp.zeros((local_groups, width + 1 - flen - 1), jnp.float32)
    one = jnp.zeros((local_groups, 1), jnp.float32)
    seq_causal = jnp.concatenate([one, taps[:, ::-1], pad], 1)
    seq_anti = jnp.concatenate([taps, pad, one], 1)
    mats_causal = split_bf16(toeplitz(seq_causal, block, width))
    mats_anti = split_bf16(toeplitz(seq_anti, block, width))

    widened = jnp.concatenate([prev_tail, product], 0)
    trailing = jnp.concatenate([grad_conv, next_head], 0)
    win_prod = windows(widened, tiles, block, width)
    win_grad = windows(trailing, tiles, block, width)

    mixed = filter_apply(mats_causal, win_prod, local_groups, per_group)
    grad_product = filter_apply(mats_anti, win_grad, local_groups, per_group)

    gc4 = grad_conv.reshape(tiles, block, local_groups, per_group)
    wp4 = win_prod.reshape(tiles, width, local_groups, per_group)
    cross = jnp.einsum("kigc,kjgc->gij", gc4, wp4, preferred_element_type=jnp.float32)
    cross = jnp.pad(cross.reshape(local_groups, block * width), ((0, 0), (0, block)))
    diag = cross.reshape(local_groups, block, width + 1)[:, :, 1 : halo + 1].sum(axis=1)
    scale = (rows * ctx_count * per_group) ** (-0.5)
    local_filters = lax.psum(diag[:, ::-1], "ctx") * scale
    grad_filters = lax.all_gather(local_filters, "mp", axis=0, tiled=True)

    grad_query = (grad_mixed * mixed).astype(jnp.bfloat16)
    grad_key = (grad_product * value_act.astype(jnp.float32)).astype(jnp.bfloat16)
    grad_value = (grad_product * key_act.astype(jnp.float32)).astype(jnp.bfloat16)
    return (grad_query, grad_key, grad_value, grad_filters)


def solution(mesh):
    in_specs = (P("ctx", "mp"), P("mp", "ctx"), P("ctx", "mp"), P("ctx", "mp"), P("ctx", "mp"), P())
    out_specs = (P("ctx", "mp"), P("ctx", "mp"), P("ctx", "mp"), P())
    return jax.shard_map(body, mesh=mesh, in_specs=in_specs, out_specs=out_specs, check_vma=False)
```

```python
import jax
import jax.numpy as jnp
from jax import lax
from jax.sharding import PartitionSpec as P


def contract(left, right):
    return lax.dot_general(
        left, right, (((1,), (1,)), ((), ())), preferred_element_type=jnp.float32
    )


def toeplitz(seq, block, width):
    groups = seq.shape[0]
    flat = jnp.tile(seq, (1, block))[:, : block * width]
    return flat.reshape(groups, block, width)


def split_bf16(x):
    hi = lax.reduce_precision(x, exponent_bits=8, mantissa_bits=7)
    lo = x - hi
    return hi.astype(jnp.bfloat16), lo.astype(jnp.bfloat16)


def windows(x, tiles, block, width):
    return jnp.stack([x[k * block : k * block + width] for k in range(tiles)])


def filter_apply(mats, wins, groups, per_group):
    tiles, width, chans = wins.shape
    w4 = wins.reshape(tiles, width, groups, per_group)
    total = None
    for m in mats:
        part = jnp.einsum("gij,kjgc->kigc", m, w4, preferred_element_type=jnp.float32)
        total = part if total is None else total + part
    block = mats[0].shape[1]
    return total.reshape(tiles * block, chans)


def body(cotangent, out_weight, query_act, key_act, value_act, filters):
    rows, chans = cotangent.shape
    groups, flen = filters.shape
    ctx_count = lax.axis_size("ctx")
    mp_count = lax.axis_size("mp")
    per_group = chans * mp_count // groups
    local_groups = chans // per_group
    halo = flen
    block = 64 if rows % 64 == 0 else rows
    tiles = rows // block
    width = block + halo

    taps = lax.dynamic_slice_in_dim(filters, lax.axis_index("mp") * local_groups, local_groups, 0)
    pad = jnp.zeros((local_groups, width + 1 - flen - 1), jnp.float32)
    one = jnp.zeros((local_groups, 1), jnp.float32)
    seq_causal = jnp.concatenate([one, taps[:, ::-1], pad], 1)
    seq_anti = jnp.concatenate([taps, pad, one], 1)
    mats_causal = split_bf16(toeplitz(seq_causal, block, width))
    mats_anti = split_bf16(toeplitz(seq_anti, block, width))

    cot_rows = lax.all_gather(cotangent, "mp", axis=1, tiled=True)
    cot_rows, mats_causal, mats_anti = lax.optimization_barrier((cot_rows, mats_causal, mats_anti))
    cot_cols = lax.all_to_all(cot_rows, "ctx", split_axis=1, concat_axis=0, tiled=True)
    partial = contract(cot_cols, out_weight)
    grad_mixed = lax.psum_scatter(partial, "ctx", scatter_dimension=0, tiled=True)

    fwd = [(k, k + 1) for k in range(ctx_count - 1)]
    bwd = [(k + 1, k) for k in range(ctx_count - 1)]
    product = (key_act.astype(jnp.float32) * value_act.astype(jnp.float32)).astype(jnp.bfloat16)
    prev_tail = lax.ppermute(product[rows - halo :], "ctx", fwd)
    widened = jnp.concatenate([prev_tail, product], 0)
    win_prod = windows(widened, tiles, block, width)
    mixed = filter_apply(mats_causal, win_prod, local_groups, per_group)
    grad_mixed, mixed = lax.optimization_barrier((grad_mixed, mixed))

    grad_conv = (grad_mixed * query_act.astype(jnp.float32)).astype(jnp.bfloat16)
    next_head = lax.ppermute(grad_conv[:halo], "ctx", bwd)
    trailing = jnp.concatenate([grad_conv, next_head], 0)
    win_grad = windows(trailing, tiles, block, width)
    grad_product = filter_apply(mats_anti, win_grad, local_groups, per_group)

    gc4 = grad_conv.reshape(tiles, block, local_groups, per_group)
    wp4 = win_prod.reshape(tiles, width, local_groups, per_group)
    cross = jnp.einsum("kigc,kjgc->gij", gc4, wp4, preferred_element_type=jnp.float32)
    cross = jnp.pad(cross.reshape(local_groups, block * width), ((0, 0), (0, block)))
    diag = cross.reshape(local_groups, block, width + 1)[:, :, 1 : halo + 1].sum(axis=1)
    scale = (rows * ctx_count * per_group) ** (-0.5)
    local_filters = lax.psum(diag[:, ::-1], "ctx") * scale
    grad_filters = lax.all_gather(local_filters, "mp", axis=0, tiled=True)

    grad_query = (grad_mixed * mixed).astype(jnp.bfloat16)
    grad_key = (grad_product * value_act.astype(jnp.float32)).astype(jnp.bfloat16)
    grad_value = (grad_product * key_act.astype(jnp.float32)).astype(jnp.bfloat16)
    return (grad_query, grad_key, grad_value, grad_filters)


def solution(mesh):
    in_specs = (P("ctx", "mp"), P("mp", "ctx"), P("ctx", "mp"), P("ctx", "mp"), P("ctx", "mp"), P())
    out_specs = (P("ctx", "mp"), P("ctx", "mp"), P("ctx", "mp"), P())
    return jax.shard_map(body, mesh=mesh, in_specs=in_specs, out_specs=out_specs, check_vma=False)
```

```python
import jax
import jax.numpy as jnp
from jax import lax
from jax.sharding import PartitionSpec as P


def contract(left, right):
    return lax.dot_general(
        left, right, (((1,), (1,)), ((), ())), preferred_element_type=jnp.float32
    )


def toeplitz(seq, block, width):
    groups = seq.shape[0]
    flat = jnp.tile(seq, (1, block))[:, : block * width]
    return flat.reshape(groups, block, width)


def split_bf16(x):
    hi = lax.reduce_precision(x, exponent_bits=8, mantissa_bits=7)
    lo = x - hi
    return hi.astype(jnp.bfloat16), lo.astype(jnp.bfloat16)


def windows(x, tiles, block, width):
    return jnp.stack([x[k * block : k * block + width] for k in range(tiles)])


def filter_apply(mats, wins, groups, per_group):
    tiles, width, chans = wins.shape
    w4 = wins.reshape(tiles, width, groups, per_group)
    total = None
    for m in mats:
        part = jnp.einsum("gij,kjgc->kigc", m, w4, preferred_element_type=jnp.float32)
        total = part if total is None else total + part
    block = mats[0].shape[1]
    return total.reshape(tiles * block, chans)


def exchange_columns(x, count):
    rows, cols = x.shape
    width = cols // count
    me = lax.axis_index("ctx")
    out = jnp.zeros((count * rows, width), x.dtype)
    own = lax.dynamic_slice_in_dim(x, me * width, width, 1)
    out = lax.dynamic_update_slice_in_dim(out, own, me * rows, 0)
    for shift in range(1, count):
        dest = (me + shift) % count
        chunk = lax.dynamic_slice_in_dim(x, dest * width, width, 1)
        got = lax.ppermute(chunk, "ctx", [(k, (k + shift) % count) for k in range(count)])
        src = (me + count - shift) % count
        out = lax.dynamic_update_slice_in_dim(out, got, src * rows, 0)
    return out


def body(cotangent, out_weight, query_act, key_act, value_act, filters):
    rows, chans = cotangent.shape
    groups, flen = filters.shape
    ctx_count = lax.axis_size("ctx")
    mp_count = lax.axis_size("mp")
    per_group = chans * mp_count // groups
    local_groups = chans // per_group
    halo = flen
    block = 64 if rows % 64 == 0 else rows
    tiles = rows // block
    width = block + halo

    taps = lax.dynamic_slice_in_dim(filters, lax.axis_index("mp") * local_groups, local_groups, 0)
    pad = jnp.zeros((local_groups, width + 1 - flen - 1), jnp.float32)
    one = jnp.zeros((local_groups, 1), jnp.float32)
    seq_causal = jnp.concatenate([one, taps[:, ::-1], pad], 1)
    seq_anti = jnp.concatenate([taps, pad, one], 1)
    mats_causal = split_bf16(toeplitz(seq_causal, block, width))
    mats_anti = split_bf16(toeplitz(seq_anti, block, width))

    cot_rows = lax.all_gather(cotangent, "mp", axis=1, tiled=True)
    cot_rows, mats_causal, mats_anti = lax.optimization_barrier((cot_rows, mats_causal, mats_anti))
    cot_cols = exchange_columns(cot_rows, ctx_count)
    partial = contract(cot_cols, out_weight)
    grad_mixed = lax.psum_scatter(partial, "ctx", scatter_dimension=0, tiled=True)

    fwd = [(k, k + 1) for k in range(ctx_count - 1)]
    bwd = [(k + 1, k) for k in range(ctx_count - 1)]
    product = (key_act.astype(jnp.float32) * value_act.astype(jnp.float32)).astype(jnp.bfloat16)
    prev_tail = lax.ppermute(product[rows - halo :], "ctx", fwd)
    widened = jnp.concatenate([prev_tail, product], 0)
    win_prod = windows(widened, tiles, block, width)
    mixed = filter_apply(mats_causal, win_prod, local_groups, per_group)
    grad_mixed, mixed = lax.optimization_barrier((grad_mixed, mixed))

    grad_conv = (grad_mixed * query_act.astype(jnp.float32)).astype(jnp.bfloat16)
    next_head = lax.ppermute(grad_conv[:halo], "ctx", bwd)
    gc4 = grad_conv.reshape(tiles, block, local_groups, per_group)
    wp4 = win_prod.reshape(tiles, width, local_groups, per_group)
    cross = jnp.einsum("kigc,kjgc->gij", gc4, wp4, preferred_element_type=jnp.float32)
    cross = jnp.pad(cross.reshape(local_groups, block * width), ((0, 0), (0, block)))
    diag = cross.reshape(local_groups, block, width + 1)[:, :, 1 : halo + 1].sum(axis=1)
    scale = (rows * ctx_count * per_group) ** (-0.5)
    diag, next_head = lax.optimization_barrier((diag, next_head))
    local_filters = lax.psum(diag[:, ::-1], "ctx") * scale
    trailing = jnp.concatenate([grad_conv, next_head], 0)
    win_grad = windows(trailing, tiles, block, width)
    grad_product = filter_apply(mats_anti, win_grad, local_groups, per_group)
    local_filters, grad_product = lax.optimization_barrier((local_filters, grad_product))

    grad_filters = lax.all_gather(local_filters, "mp", axis=0, tiled=True)

    grad_query = (grad_mixed * mixed).astype(jnp.bfloat16)
    grad_key = (grad_product * value_act.astype(jnp.float32)).astype(jnp.bfloat16)
    grad_value = (grad_product * key_act.astype(jnp.float32)).astype(jnp.bfloat16)
    return (grad_query, grad_key, grad_value, grad_filters)


def solution(mesh):
    in_specs = (P("ctx", "mp"), P("mp", "ctx"), P("ctx", "mp"), P("ctx", "mp"), P("ctx", "mp"), P())
    out_specs = (P("ctx", "mp"), P("ctx", "mp"), P("ctx", "mp"), P())
    return jax.shard_map(body, mesh=mesh, in_specs=in_specs, out_specs=out_specs, check_vma=False)
```

```python
import jax
import jax.numpy as jnp
from jax import lax
from jax.sharding import PartitionSpec as P


def contract(left, right):
    return lax.dot_general(
        left, right, (((1,), (1,)), ((), ())), preferred_element_type=jnp.float32
    )


def toeplitz(seq, block, width):
    groups = seq.shape[0]
    flat = jnp.tile(seq, (1, block))[:, : block * width]
    return flat.reshape(groups, block, width)


def split_bf16(x):
    hi = lax.reduce_precision(x, exponent_bits=8, mantissa_bits=7)
    lo = x - hi
    return hi.astype(jnp.bfloat16), lo.astype(jnp.bfloat16)


def windows(x, tiles, block, width):
    return jnp.stack([x[k * block : k * block + width] for k in range(tiles)])


def filter_apply(mats, wins, groups, per_group):
    tiles, width, chans = wins.shape
    w4 = wins.reshape(tiles, width, groups, per_group)
    total = None
    for m in mats:
        part = jnp.einsum("gij,kjgc->kigc", m, w4, preferred_element_type=jnp.float32)
        total = part if total is None else total + part
    block = mats[0].shape[1]
    return total.reshape(tiles * block, chans)


def exchange_columns(x, count):
    rows, cols = x.shape
    width = cols // count
    me = lax.axis_index("ctx")
    out = jnp.zeros((count * rows, width), x.dtype)
    own = lax.dynamic_slice_in_dim(x, me * width, width, 1)
    out = lax.dynamic_update_slice_in_dim(out, own, me * rows, 0)
    for shift in range(1, count):
        dest = (me + shift) % count
        chunk = lax.dynamic_slice_in_dim(x, dest * width, width, 1)
        got = lax.ppermute(chunk, "ctx", [(k, (k + shift) % count) for k in range(count)])
        src = (me + count - shift) % count
        out = lax.dynamic_update_slice_in_dim(out, got, src * rows, 0)
    return out


def butterfly_sum(x, axis, count):
    if count & (count - 1):
        return lax.psum(x, axis)
    step = 1
    while step < count:
        x = x + lax.ppermute(x, axis, [(k, k ^ step) for k in range(count)])
        step *= 2
    return x


def butterfly_gather(x, axis, count):
    if count & (count - 1):
        return lax.all_gather(x, axis, axis=0, tiled=True)
    me = lax.axis_index(axis)
    step = 1
    while step < count:
        got = lax.ppermute(x, axis, [(k, k ^ step) for k in range(count)])
        low = (me // step) % 2 == 0
        x = jnp.where(low, jnp.concatenate([x, got]), jnp.concatenate([got, x]))
        step *= 2
    return x


def body(cotangent, out_weight, query_act, key_act, value_act, filters):
    rows, chans = cotangent.shape
    groups, flen = filters.shape
    ctx_count = lax.axis_size("ctx")
    mp_count = lax.axis_size("mp")
    per_group = chans * mp_count // groups
    local_groups = chans // per_group
    halo = flen
    block = 64 if rows % 64 == 0 else rows
    tiles = rows // block
    width = block + halo

    taps = lax.dynamic_slice_in_dim(filters, lax.axis_index("mp") * local_groups, local_groups, 0)
    pad = jnp.zeros((local_groups, width + 1 - flen - 1), jnp.float32)
    one = jnp.zeros((local_groups, 1), jnp.float32)
    seq_causal = jnp.concatenate([one, taps[:, ::-1], pad], 1)
    seq_anti = jnp.concatenate([taps, pad, one], 1)
    mats_causal = split_bf16(toeplitz(seq_causal, block, width))
    mats_anti = split_bf16(toeplitz(seq_anti, block, width))

    cot_rows = lax.all_gather(cotangent, "mp", axis=1, tiled=True)
    cot_rows, mats_causal, mats_anti = lax.optimization_barrier((cot_rows, mats_causal, mats_anti))
    cot_cols = exchange_columns(cot_rows, ctx_count)
    partial = contract(cot_cols, out_weight)
    grad_mixed = lax.psum_scatter(partial, "ctx", scatter_dimension=0, tiled=True)

    fwd = [(k, k + 1) for k in range(ctx_count - 1)]
    bwd = [(k + 1, k) for k in range(ctx_count - 1)]
    product = (key_act.astype(jnp.float32) * value_act.astype(jnp.float32)).astype(jnp.bfloat16)
    prev_tail = lax.ppermute(product[rows - halo :], "ctx", fwd)
    widened = jnp.concatenate([prev_tail, product], 0)
    win_prod = windows(widened, tiles, block, width)
    mixed = filter_apply(mats_causal, win_prod, local_groups, per_group)
    grad_mixed, mixed = lax.optimization_barrier((grad_mixed, mixed))

    grad_conv = (grad_mixed * query_act.astype(jnp.float32)).astype(jnp.bfloat16)
    next_head = lax.ppermute(grad_conv[:halo], "ctx", bwd)
    gc4 = grad_conv.reshape(tiles, block, local_groups, per_group)
    wp4 = win_prod.reshape(tiles, width, local_groups, per_group)
    cross = jnp.einsum("kigc,kjgc->gij", gc4, wp4, preferred_element_type=jnp.float32)
    cross = jnp.pad(cross.reshape(local_groups, block * width), ((0, 0), (0, block)))
    diag = cross.reshape(local_groups, block, width + 1)[:, :, 1 : halo + 1].sum(axis=1)
    scale = (rows * ctx_count * per_group) ** (-0.5)
    diag, next_head = lax.optimization_barrier((diag, next_head))
    local_filters = butterfly_sum(diag[:, ::-1], "ctx", ctx_count) * scale
    grad_filters = butterfly_gather(local_filters, "mp", mp_count)
    trailing = jnp.concatenate([grad_conv, next_head], 0)
    win_grad = windows(trailing, tiles, block, width)
    grad_product = filter_apply(mats_anti, win_grad, local_groups, per_group)
    grad_filters, grad_product = lax.optimization_barrier((grad_filters, grad_product))


    grad_query = (grad_mixed * mixed).astype(jnp.bfloat16)
    grad_key = (grad_product * value_act.astype(jnp.float32)).astype(jnp.bfloat16)
    grad_value = (grad_product * key_act.astype(jnp.float32)).astype(jnp.bfloat16)
    return (grad_query, grad_key, grad_value, grad_filters)


def solution(mesh):
    in_specs = (P("ctx", "mp"), P("mp", "ctx"), P("ctx", "mp"), P("ctx", "mp"), P("ctx", "mp"), P())
    out_specs = (P("ctx", "mp"), P("ctx", "mp"), P("ctx", "mp"), P())
    return jax.shard_map(body, mesh=mesh, in_specs=in_specs, out_specs=out_specs, check_vma=False)
```

```python
import jax
import jax.numpy as jnp
from jax import lax
from jax.sharding import PartitionSpec as P


def contract(left, right):
    return lax.dot_general(
        left, right, (((1,), (1,)), ((), ())), preferred_element_type=jnp.float32
    )


def toeplitz(seq, block, width):
    groups = seq.shape[0]
    flat = jnp.tile(seq, (1, block))[:, : block * width]
    return flat.reshape(groups, block, width)


def split_bf16(x):
    hi = lax.reduce_precision(x, exponent_bits=8, mantissa_bits=7)
    lo = x - hi
    return hi.astype(jnp.bfloat16), lo.astype(jnp.bfloat16)


def windows(x, tiles, block, width):
    return jnp.stack([x[k * block : k * block + width] for k in range(tiles)])


def filter_apply(mats, wins, groups, per_group):
    tiles, width, chans = wins.shape
    w4 = wins.reshape(tiles, width, groups, per_group)
    total = None
    for m in mats:
        part = jnp.einsum("gij,kjgc->kigc", m, w4, preferred_element_type=jnp.float32)
        total = part if total is None else total + part
    block = mats[0].shape[1]
    return total.reshape(tiles * block, chans)


def exchange_columns(x, count):
    rows, cols = x.shape
    width = cols // count
    me = lax.axis_index("ctx")
    out = jnp.zeros((count * rows, width), x.dtype)
    own = lax.dynamic_slice_in_dim(x, me * width, width, 1)
    out = lax.dynamic_update_slice_in_dim(out, own, me * rows, 0)
    for shift in range(1, count):
        dest = (me + shift) % count
        chunk = lax.dynamic_slice_in_dim(x, dest * width, width, 1)
        got = lax.ppermute(chunk, "ctx", [(k, (k + shift) % count) for k in range(count)])
        src = (me + count - shift) % count
        out = lax.dynamic_update_slice_in_dim(out, got, src * rows, 0)
    return out


def butterfly_sum(x, axis, count):
    if count & (count - 1):
        return lax.psum(x, axis)
    step = 1
    while step < count:
        x = x + lax.ppermute(x, axis, [(k, k ^ step) for k in range(count)])
        step *= 2
    return x


def butterfly_gather(x, axis, count):
    if count & (count - 1):
        return lax.all_gather(x, axis, axis=0, tiled=True)
    me = lax.axis_index(axis)
    step = 1
    while step < count:
        got = lax.ppermute(x, axis, [(k, k ^ step) for k in range(count)])
        low = (me // step) % 2 == 0
        x = jnp.where(low, jnp.concatenate([x, got]), jnp.concatenate([got, x]))
        step *= 2
    return x


def body(cotangent, out_weight, query_act, key_act, value_act, filters):
    rows, chans = cotangent.shape
    groups, flen = filters.shape
    ctx_count = lax.axis_size("ctx")
    mp_count = lax.axis_size("mp")
    per_group = chans * mp_count // groups
    local_groups = chans // per_group
    halo = flen
    block = 64 if rows % 64 == 0 else rows
    tiles = rows // block
    width = block + halo

    taps = lax.dynamic_slice_in_dim(filters, lax.axis_index("mp") * local_groups, local_groups, 0)
    pad = jnp.zeros((local_groups, width + 1 - flen - 1), jnp.float32)
    one = jnp.zeros((local_groups, 1), jnp.float32)
    seq_causal = jnp.concatenate([one, taps[:, ::-1], pad], 1)
    mats_causal = split_bf16(toeplitz(seq_causal, block, width))

    cot_rows = lax.all_gather(cotangent, "mp", axis=1, tiled=True)
    cot_rows, mats_causal = lax.optimization_barrier((cot_rows, mats_causal))
    cot_cols = exchange_columns(cot_rows, ctx_count)
    partial = contract(cot_cols, out_weight)
    grad_mixed = lax.psum_scatter(partial, "ctx", scatter_dimension=0, tiled=True)

    fwd = [(k, k + 1) for k in range(ctx_count - 1)]
    bwd = [(k + 1, k) for k in range(ctx_count - 1)]
    product = (key_act.astype(jnp.float32) * value_act.astype(jnp.float32)).astype(jnp.bfloat16)
    prev_tail = lax.ppermute(product[rows - halo :], "ctx", fwd)
    widened = jnp.concatenate([prev_tail, product], 0)
    win_prod = windows(widened, tiles, block, width)
    mixed = filter_apply(mats_causal, win_prod, local_groups, per_group)
    grad_mixed, mixed = lax.optimization_barrier((grad_mixed, mixed))

    grad_conv = (grad_mixed * query_act.astype(jnp.float32)).astype(jnp.bfloat16)
    next_head = lax.ppermute(grad_conv[:halo], "ctx", bwd)
    gc4 = grad_conv.reshape(tiles, block, local_groups, per_group)
    wp4 = win_prod.reshape(tiles, width, local_groups, per_group)
    cross = jnp.einsum("kigc,kjgc->gij", gc4, wp4, preferred_element_type=jnp.float32)
    cross = jnp.pad(cross.reshape(local_groups, block * width), ((0, 0), (0, block)))
    diag = cross.reshape(local_groups, block, width + 1)[:, :, 1 : halo + 1].sum(axis=1)
    scale = (rows * ctx_count * per_group) ** (-0.5)
    diag, next_head = lax.optimization_barrier((diag, next_head))
    local_filters = butterfly_sum(diag[:, ::-1], "ctx", ctx_count) * scale
    grad_filters = butterfly_gather(local_filters, "mp", mp_count)
    trailing = jnp.concatenate([next_head[::-1], grad_conv[::-1]], 0)
    win_grad = windows(trailing, tiles, block, width)
    grad_product = filter_apply(mats_causal, win_grad, local_groups, per_group)[::-1]
    grad_filters, grad_product = lax.optimization_barrier((grad_filters, grad_product))


    grad_query = (grad_mixed * mixed).astype(jnp.bfloat16)
    grad_key = (grad_product * value_act.astype(jnp.float32)).astype(jnp.bfloat16)
    grad_value = (grad_product * key_act.astype(jnp.float32)).astype(jnp.bfloat16)
    return (grad_query, grad_key, grad_value, grad_filters)


def solution(mesh):
    in_specs = (P("ctx", "mp"), P("mp", "ctx"), P("ctx", "mp"), P("ctx", "mp"), P("ctx", "mp"), P())
    out_specs = (P("ctx", "mp"), P("ctx", "mp"), P("ctx", "mp"), P())
    return jax.shard_map(body, mesh=mesh, in_specs=in_specs, out_specs=out_specs, check_vma=False)
```

```python
import jax
import jax.numpy as jnp
from jax import lax
from jax.sharding import PartitionSpec as P


def contract(left, right):
    return lax.dot_general(
        left, right, (((1,), (1,)), ((), ())), preferred_element_type=jnp.float32
    )


def toeplitz(seq, block, width):
    groups = seq.shape[0]
    flat = jnp.tile(seq, (1, block))[:, : block * width]
    return flat.reshape(groups, block, width)


def split_bf16(x):
    hi = lax.reduce_precision(x, exponent_bits=8, mantissa_bits=7)
    lo = x - hi
    return hi.astype(jnp.bfloat16), lo.astype(jnp.bfloat16)


def windows(x, tiles, block, width):
    return jnp.stack([x[k * block : k * block + width] for k in range(tiles)])


def filter_apply(mats, wins, groups, per_group):
    tiles, width, chans = wins.shape
    w4 = wins.reshape(tiles, width, groups, per_group)
    total = None
    for m in mats:
        part = jnp.einsum("gij,kjgc->kigc", m, w4, preferred_element_type=jnp.float32)
        total = part if total is None else total + part
    block = mats[0].shape[1]
    return total.reshape(tiles * block, chans)


def exchange_columns(x, count):
    rows, cols = x.shape
    width = cols // count
    me = lax.axis_index("ctx")
    out = jnp.zeros((count * rows, width), x.dtype)
    own = lax.dynamic_slice_in_dim(x, me * width, width, 1)
    out = lax.dynamic_update_slice_in_dim(out, own, me * rows, 0)
    for shift in range(1, count):
        dest = (me + shift) % count
        chunk = lax.dynamic_slice_in_dim(x, dest * width, width, 1)
        got = lax.ppermute(chunk, "ctx", [(k, (k + shift) % count) for k in range(count)])
        src = (me + count - shift) % count
        out = lax.dynamic_update_slice_in_dim(out, got, src * rows, 0)
    return out


def butterfly_sum(x, axis, count):
    if count & (count - 1):
        return lax.psum(x, axis)
    step = 1
    while step < count:
        x = x + lax.ppermute(x, axis, [(k, k ^ step) for k in range(count)])
        step *= 2
    return x


def butterfly_gather(x, axis, count):
    if count & (count - 1):
        return lax.all_gather(x, axis, axis=0, tiled=True)
    me = lax.axis_index(axis)
    step = 1
    while step < count:
        got = lax.ppermute(x, axis, [(k, k ^ step) for k in range(count)])
        low = (me // step) % 2 == 0
        x = jnp.where(low, jnp.concatenate([x, got]), jnp.concatenate([got, x]))
        step *= 2
    return x


def body(cotangent, out_weight, query_act, key_act, value_act, filters):
    rows, chans = cotangent.shape
    groups, flen = filters.shape
    ctx_count = lax.axis_size("ctx")
    mp_count = lax.axis_size("mp")
    per_group = chans * mp_count // groups
    local_groups = chans // per_group
    halo = flen
    block = 64 if rows % 64 == 0 else rows
    tiles = rows // block
    width = block + halo

    taps = lax.dynamic_slice_in_dim(filters, lax.axis_index("mp") * local_groups, local_groups, 0)
    pad = jnp.zeros((local_groups, width + 1 - flen - 1), jnp.float32)
    one = jnp.zeros((local_groups, 1), jnp.float32)
    seq_causal = jnp.concatenate([one, taps[:, ::-1], pad], 1)
    seq_anti = jnp.concatenate([taps, pad, one], 1)
    mats_causal = split_bf16(toeplitz(seq_causal, block, width))
    mats_anti = split_bf16(toeplitz(seq_anti, block, width))

    cot_rows = lax.all_gather(cotangent, "mp", axis=1, tiled=True)
    cot_rows, mats_causal, mats_anti = lax.optimization_barrier((cot_rows, mats_causal, mats_anti))
    cot_cols = exchange_columns(cot_rows, ctx_count)
    chunks = 2 if local_groups % 2 == 0 else 1
    chunk_groups = local_groups // chunks
    chunk_chans = chans // chunks
    grad_parts = []
    for h in range(chunks):
        partial = contract(cot_cols, out_weight[h * chunk_chans : (h + 1) * chunk_chans])
        grad_parts.append(lax.psum_scatter(partial, "ctx", scatter_dimension=0, tiled=True))

    fwd = [(k, k + 1) for k in range(ctx_count - 1)]
    bwd = [(k + 1, k) for k in range(ctx_count - 1)]
    product = (key_act.astype(jnp.float32) * value_act.astype(jnp.float32)).astype(jnp.bfloat16)
    prev_tail = lax.ppermute(product[rows - halo :], "ctx", fwd)
    widened = jnp.concatenate([prev_tail, product], 0)
    win_prod = windows(widened, tiles, block, width)

    def cut(x, h):
        return x[..., h * chunk_chans : (h + 1) * chunk_chans]

    mats_parts = [tuple(m[h * chunk_groups : (h + 1) * chunk_groups] for m in mats_causal) for h in range(chunks)]
    anti_parts = [tuple(m[h * chunk_groups : (h + 1) * chunk_groups] for m in mats_anti) for h in range(chunks)]
    mixed_parts = [filter_apply(mats_parts[h], cut(win_prod, h), chunk_groups, per_group) for h in range(chunks)]
    grad_parts[0], mixed_parts = lax.optimization_barrier((grad_parts[0], mixed_parts))

    scale = (rows * ctx_count * per_group) ** (-0.5)
    outs = []
    diags = []
    for h in range(chunks):
        grad_mixed = grad_parts[h]
        grad_conv = (grad_mixed * cut(query_act, h).astype(jnp.float32)).astype(jnp.bfloat16)
        next_head = lax.ppermute(grad_conv[:halo], "ctx", bwd)
        gc4 = grad_conv.reshape(tiles, block, chunk_groups, per_group)
        wp4 = cut(win_prod, h).reshape(tiles, width, chunk_groups, per_group)
        cross = jnp.einsum("kigc,kjgc->gij", gc4, wp4, preferred_element_type=jnp.float32)
        cross = jnp.pad(cross.reshape(chunk_groups, block * width), ((0, 0), (0, block)))
        diag = cross.reshape(chunk_groups, block, width + 1)[:, :, 1 : halo + 1].sum(axis=1)
        diag, next_head = lax.optimization_barrier((diag, next_head))
        diags.append(diag)
        if h == chunks - 1:
            local_filters = butterfly_sum(jnp.concatenate(diags, 0)[:, ::-1], "ctx", ctx_count) * scale
            grad_filters = butterfly_gather(local_filters, "mp", mp_count)
        trailing = jnp.concatenate([grad_conv, next_head], 0)
        win_grad = windows(trailing, tiles, block, width)
        grad_product = filter_apply(anti_parts[h], win_grad, chunk_groups, per_group)
        mixed = mixed_parts[h]
        grad_query = (grad_mixed * mixed).astype(jnp.bfloat16)
        grad_key = (grad_product * cut(value_act, h).astype(jnp.float32)).astype(jnp.bfloat16)
        grad_value = (grad_product * cut(key_act, h).astype(jnp.float32)).astype(jnp.bfloat16)
        part = (grad_query, grad_key, grad_value)
        if h + 1 < chunks:
            grad_parts[h + 1], part = lax.optimization_barrier((grad_parts[h + 1], part))
        else:
            grad_filters, part = lax.optimization_barrier((grad_filters, part))
        outs.append(part)
    grad_query, grad_key, grad_value = (jnp.concatenate([o[n] for o in outs], 1) for n in range(3))
    return (grad_query, grad_key, grad_value, grad_filters)


def solution(mesh):
    in_specs = (P("ctx", "mp"), P("mp", "ctx"), P("ctx", "mp"), P("ctx", "mp"), P("ctx", "mp"), P())
    out_specs = (P("ctx", "mp"), P("ctx", "mp"), P("ctx", "mp"), P())
    return jax.shard_map(body, mesh=mesh, in_specs=in_specs, out_specs=out_specs, check_vma=False)
```

```python
import jax
import jax.numpy as jnp
from jax import lax
from jax.sharding import PartitionSpec as P


def contract(left, right):
    return lax.dot_general(
        left, right, (((1,), (1,)), ((), ())), preferred_element_type=jnp.float32
    )


def toeplitz(seq, block, width):
    groups = seq.shape[0]
    flat = jnp.tile(seq, (1, block))[:, : block * width]
    return flat.reshape(groups, block, width)


def toeplitz_mats(taps, block, width, halo, causal, zero):
    groups, flen = taps.shape
    hi = lax.reduce_precision(taps, exponent_bits=8, mantissa_bits=7)
    both = jnp.concatenate([hi, taps - hi], 0).astype(jnp.bfloat16)
    i = lax.broadcasted_iota(jnp.int32, (block, width, flen), 0)
    j = lax.broadcasted_iota(jnp.int32, (block, width, flen), 1)
    s = lax.broadcasted_iota(jnp.int32, (block, width, flen), 2) + zero
    lag = i + halo - j if causal else j - i
    pick = (lag == s).astype(jnp.bfloat16)
    mats = jnp.einsum("gs,ijs->gij", both, pick, preferred_element_type=jnp.float32)
    mats = mats.astype(jnp.bfloat16)
    return mats[:groups], mats[groups:]


def split_bf16(x):
    hi = lax.reduce_precision(x, exponent_bits=8, mantissa_bits=7)
    lo = x - hi
    return hi.astype(jnp.bfloat16), lo.astype(jnp.bfloat16)


def windows(x, tiles, block, width):
    return jnp.stack([x[k * block : k * block + width] for k in range(tiles)])


def filter_apply(mats, wins, groups, per_group):
    tiles, width, chans = wins.shape
    w4 = wins.reshape(tiles, width, groups, per_group)
    total = None
    for m in mats:
        part = jnp.einsum("gij,kjgc->kigc", m, w4, preferred_element_type=jnp.float32)
        total = part if total is None else total + part
    block = mats[0].shape[1]
    return total.reshape(tiles * block, chans)


def exchange_columns(x, count):
    rows, cols = x.shape
    width = cols // count
    me = lax.axis_index("ctx")
    out = jnp.zeros((count * rows, width), x.dtype)
    own = lax.dynamic_slice_in_dim(x, me * width, width, 1)
    out = lax.dynamic_update_slice_in_dim(out, own, me * rows, 0)
    for shift in range(1, count):
        dest = (me + shift) % count
        chunk = lax.dynamic_slice_in_dim(x, dest * width, width, 1)
        got = lax.ppermute(chunk, "ctx", [(k, (k + shift) % count) for k in range(count)])
        src = (me + count - shift) % count
        out = lax.dynamic_update_slice_in_dim(out, got, src * rows, 0)
    return out


def butterfly_sum(x, axis, count):
    if count & (count - 1):
        return lax.psum(x, axis)
    step = 1
    while step < count:
        x = x + lax.ppermute(x, axis, [(k, k ^ step) for k in range(count)])
        step *= 2
    return x


def butterfly_gather(x, axis, count):
    if count & (count - 1):
        return lax.all_gather(x, axis, axis=0, tiled=True)
    me = lax.axis_index(axis)
    step = 1
    while step < count:
        got = lax.ppermute(x, axis, [(k, k ^ step) for k in range(count)])
        low = (me // step) % 2 == 0
        x = jnp.where(low, jnp.concatenate([x, got]), jnp.concatenate([got, x]))
        step *= 2
    return x


def body(cotangent, out_weight, query_act, key_act, value_act, filters):
    rows, chans = cotangent.shape
    groups, flen = filters.shape
    ctx_count = lax.axis_size("ctx")
    mp_count = lax.axis_size("mp")
    per_group = chans * mp_count // groups
    local_groups = chans // per_group
    halo = flen
    block = 64 if rows % 64 == 0 else rows
    tiles = rows // block
    width = block + halo

    taps = lax.dynamic_slice_in_dim(filters, lax.axis_index("mp") * local_groups, local_groups, 0)
    pad = jnp.zeros((local_groups, width + 1 - flen - 1), jnp.float32)
    one = jnp.zeros((local_groups, 1), jnp.float32)
    seq_causal = jnp.concatenate([one, taps[:, ::-1], pad], 1)
    seq_anti = jnp.concatenate([taps, pad, one], 1)
    zero = lax.axis_index("ctx") // ctx_count
    mats_causal = toeplitz_mats(taps, block, width, halo, True, zero)
    mats_anti = toeplitz_mats(taps, block, width, halo, False, zero)

    cot_rows = lax.all_gather(cotangent, "mp", axis=1, tiled=True)
    cot_rows, mats_causal, mats_anti = lax.optimization_barrier((cot_rows, mats_causal, mats_anti))
    cot_cols = exchange_columns(cot_rows, ctx_count)
    partial = contract(cot_cols, out_weight)
    grad_mixed = lax.psum_scatter(partial, "ctx", scatter_dimension=0, tiled=True)

    fwd = [(k, k + 1) for k in range(ctx_count - 1)]
    bwd = [(k + 1, k) for k in range(ctx_count - 1)]
    product = (key_act.astype(jnp.float32) * value_act.astype(jnp.float32)).astype(jnp.bfloat16)
    prev_tail = lax.ppermute(product[rows - halo :], "ctx", fwd)
    widened = jnp.concatenate([prev_tail, product], 0)
    win_prod = windows(widened, tiles, block, width)
    mixed = filter_apply(mats_causal, win_prod, local_groups, per_group)
    grad_mixed, mixed = lax.optimization_barrier((grad_mixed, mixed))

    grad_conv = (grad_mixed * query_act.astype(jnp.float32)).astype(jnp.bfloat16)
    next_head = lax.ppermute(grad_conv[:halo], "ctx", bwd)
    gc4 = grad_conv.reshape(tiles, block, local_groups, per_group)
    wp4 = win_prod.reshape(tiles, width, local_groups, per_group)
    cross = jnp.einsum("kigc,kjgc->gij", gc4, wp4, preferred_element_type=jnp.float32)
    cross = jnp.pad(cross.reshape(local_groups, block * width), ((0, 0), (0, block)))
    diag = cross.reshape(local_groups, block, width + 1)[:, :, 1 : halo + 1].sum(axis=1)
    scale = (rows * ctx_count * per_group) ** (-0.5)
    diag, next_head = lax.optimization_barrier((diag, next_head))
    local_filters = butterfly_sum(diag[:, ::-1], "ctx", ctx_count) * scale
    grad_filters = butterfly_gather(local_filters, "mp", mp_count)
    trailing = jnp.concatenate([grad_conv, next_head], 0)
    win_grad = windows(trailing, tiles, block, width)
    grad_product = filter_apply(mats_anti, win_grad, local_groups, per_group)
    grad_filters, grad_product = lax.optimization_barrier((grad_filters, grad_product))


    grad_query = (grad_mixed * mixed).astype(jnp.bfloat16)
    grad_key = (grad_product * value_act.astype(jnp.float32)).astype(jnp.bfloat16)
    grad_value = (grad_product * key_act.astype(jnp.float32)).astype(jnp.bfloat16)
    return (grad_query, grad_key, grad_value, grad_filters)


def solution(mesh):
    in_specs = (P("ctx", "mp"), P("mp", "ctx"), P("ctx", "mp"), P("ctx", "mp"), P("ctx", "mp"), P())
    out_specs = (P("ctx", "mp"), P("ctx", "mp"), P("ctx", "mp"), P())
    return jax.shard_map(body, mesh=mesh, in_specs=in_specs, out_specs=out_specs, check_vma=False)
```

```python
import jax
import jax.numpy as jnp
from jax import lax
from jax.sharding import PartitionSpec as P


def contract(left, right):
    return lax.dot_general(
        left, right, (((1,), (1,)), ((), ())), preferred_element_type=jnp.float32
    )


def toeplitz(seq, block, width):
    groups = seq.shape[0]
    flat = jnp.tile(seq, (1, block))[:, : block * width]
    return flat.reshape(groups, block, width)


def toeplitz_mats(taps, block, width, halo, causal, zero):
    groups, flen = taps.shape
    hi = lax.reduce_precision(taps, exponent_bits=8, mantissa_bits=7)
    both = jnp.concatenate([hi, taps - hi], 0).astype(jnp.bfloat16)
    i = lax.broadcasted_iota(jnp.int32, (block, width, flen), 0)
    j = lax.broadcasted_iota(jnp.int32, (block, width, flen), 1)
    s = lax.broadcasted_iota(jnp.int32, (block, width, flen), 2) + zero
    lag = i + halo - j if causal else j - i
    pick = (lag == s).astype(jnp.bfloat16)
    mats = jnp.einsum("gs,ijs->gij", both, pick, preferred_element_type=jnp.float32)
    mats = mats.astype(jnp.bfloat16)
    return mats[:groups], mats[groups:]


def split_bf16(x):
    hi = lax.reduce_precision(x, exponent_bits=8, mantissa_bits=7)
    lo = x - hi
    return hi.astype(jnp.bfloat16), lo.astype(jnp.bfloat16)


def windows(x, tiles, block, width):
    return jnp.stack([x[k * block : k * block + width] for k in range(tiles)])


def filter_apply(mats, wins, groups, per_group):
    tiles, width, chans = wins.shape
    w4 = wins.reshape(tiles, width, groups, per_group)
    total = None
    for m in mats:
        part = jnp.einsum("gij,kjgc->kigc", m, w4, preferred_element_type=jnp.float32)
        total = part if total is None else total + part
    block = mats[0].shape[1]
    return total.reshape(tiles * block, chans)


def exchange_columns(x, count):
    rows, cols = x.shape
    width = cols // count
    me = lax.axis_index("ctx")
    out = jnp.zeros((count * rows, width), x.dtype)
    own = lax.dynamic_slice_in_dim(x, me * width, width, 1)
    out = lax.dynamic_update_slice_in_dim(out, own, me * rows, 0)
    for shift in range(1, count):
        dest = (me + shift) % count
        chunk = lax.dynamic_slice_in_dim(x, dest * width, width, 1)
        got = lax.ppermute(chunk, "ctx", [(k, (k + shift) % count) for k in range(count)])
        src = (me + count - shift) % count
        out = lax.dynamic_update_slice_in_dim(out, got, src * rows, 0)
    return out


def butterfly_sum(x, axis, count):
    if count & (count - 1):
        return lax.psum(x, axis)
    step = 1
    while step < count:
        x = x + lax.ppermute(x, axis, [(k, k ^ step) for k in range(count)])
        step *= 2
    return x


def butterfly_gather(x, axis, count):
    if count & (count - 1):
        return lax.all_gather(x, axis, axis=0, tiled=True)
    me = lax.axis_index(axis)
    step = 1
    while step < count:
        got = lax.ppermute(x, axis, [(k, k ^ step) for k in range(count)])
        low = (me // step) % 2 == 0
        x = jnp.where(low, jnp.concatenate([x, got]), jnp.concatenate([got, x]))
        step *= 2
    return x


def gather_columns(x, axis, count):
    rows, cols = x.shape
    me = lax.axis_index(axis)
    out = jnp.zeros((rows, count * cols), x.dtype)
    out = lax.dynamic_update_slice_in_dim(out, x, me * cols, 1)
    for shift in range(1, count):
        got = lax.ppermute(x, axis, [(k, (k + shift) % count) for k in range(count)])
        src = (me + count - shift) % count
        out = lax.dynamic_update_slice_in_dim(out, got, src * cols, 1)
    return out


def body(cotangent, out_weight, query_act, key_act, value_act, filters):
    rows, chans = cotangent.shape
    groups, flen = filters.shape
    ctx_count = lax.axis_size("ctx")
    mp_count = lax.axis_size("mp")
    per_group = chans * mp_count // groups
    local_groups = chans // per_group
    halo = flen
    block = 64 if rows % 64 == 0 else rows
    tiles = rows // block
    width = block + halo

    taps = lax.dynamic_slice_in_dim(filters, lax.axis_index("mp") * local_groups, local_groups, 0)
    pad = jnp.zeros((local_groups, width + 1 - flen - 1), jnp.float32)
    one = jnp.zeros((local_groups, 1), jnp.float32)
    seq_causal = jnp.concatenate([one, taps[:, ::-1], pad], 1)
    seq_anti = jnp.concatenate([taps, pad, one], 1)
    zero = lax.axis_index("ctx") // ctx_count
    mats_causal = toeplitz_mats(taps, block, width, halo, True, zero)
    mats_anti = toeplitz_mats(taps, block, width, halo, False, zero)

    cot_rows = gather_columns(cotangent, "mp", mp_count)
    cot_rows, mats_causal, mats_anti = lax.optimization_barrier((cot_rows, mats_causal, mats_anti))
    cot_cols = exchange_columns(cot_rows, ctx_count)
    partial = contract(cot_cols, out_weight)
    grad_mixed = lax.psum_scatter(partial, "ctx", scatter_dimension=0, tiled=True)

    fwd = [(k, k + 1) for k in range(ctx_count - 1)]
    bwd = [(k + 1, k) for k in range(ctx_count - 1)]
    product = (key_act.astype(jnp.float32) * value_act.astype(jnp.float32)).astype(jnp.bfloat16)
    prev_tail = lax.ppermute(product[rows - halo :], "ctx", fwd)
    widened = jnp.concatenate([prev_tail, product], 0)
    win_prod = windows(widened, tiles, block, width)
    mixed = filter_apply(mats_causal, win_prod, local_groups, per_group)
    grad_mixed, mixed = lax.optimization_barrier((grad_mixed, mixed))

    grad_conv = (grad_mixed * query_act.astype(jnp.float32)).astype(jnp.bfloat16)
    next_head = lax.ppermute(grad_conv[:halo], "ctx", bwd)
    gc4 = grad_conv.reshape(tiles, block, local_groups, per_group)
    wp4 = win_prod.reshape(tiles, width, local_groups, per_group)
    cross = jnp.einsum("kigc,kjgc->gij", gc4, wp4, preferred_element_type=jnp.float32)
    cross = jnp.pad(cross.reshape(local_groups, block * width), ((0, 0), (0, block)))
    diag = cross.reshape(local_groups, block, width + 1)[:, :, 1 : halo + 1].sum(axis=1)
    scale = (rows * ctx_count * per_group) ** (-0.5)
    diag, next_head = lax.optimization_barrier((diag, next_head))
    local_filters = butterfly_sum(diag[:, ::-1], "ctx", ctx_count) * scale
    grad_filters = butterfly_gather(local_filters, "mp", mp_count)
    trailing = jnp.concatenate([grad_conv, next_head], 0)
    win_grad = windows(trailing, tiles, block, width)
    grad_product = filter_apply(mats_anti, win_grad, local_groups, per_group)
    grad_filters, grad_product = lax.optimization_barrier((grad_filters, grad_product))


    grad_query = (grad_mixed * mixed).astype(jnp.bfloat16)
    grad_key = (grad_product * value_act.astype(jnp.float32)).astype(jnp.bfloat16)
    grad_value = (grad_product * key_act.astype(jnp.float32)).astype(jnp.bfloat16)
    return (grad_query, grad_key, grad_value, grad_filters)


def solution(mesh):
    in_specs = (P("ctx", "mp"), P("mp", "ctx"), P("ctx", "mp"), P("ctx", "mp"), P("ctx", "mp"), P())
    out_specs = (P("ctx", "mp"), P("ctx", "mp"), P("ctx", "mp"), P())
    return jax.shard_map(body, mesh=mesh, in_specs=in_specs, out_specs=out_specs, check_vma=False)
```

```python
import jax
import jax.numpy as jnp
from jax import lax
from jax.sharding import PartitionSpec as P


def contract(left, right):
    return lax.dot_general(
        left, right, (((1,), (1,)), ((), ())), preferred_element_type=jnp.float32
    )


def toeplitz(seq, block, width):
    groups = seq.shape[0]
    flat = jnp.tile(seq, (1, block))[:, : block * width]
    return flat.reshape(groups, block, width)


def toeplitz_mats(taps, block, width, halo, causal, zero):
    groups, flen = taps.shape
    hi = lax.reduce_precision(taps, exponent_bits=8, mantissa_bits=7)
    both = jnp.concatenate([hi, taps - hi], 0).astype(jnp.bfloat16)
    i = lax.broadcasted_iota(jnp.int32, (block, width, flen), 0)
    j = lax.broadcasted_iota(jnp.int32, (block, width, flen), 1)
    s = lax.broadcasted_iota(jnp.int32, (block, width, flen), 2) + zero
    lag = i + halo - j if causal else j - i
    pick = (lag == s).astype(jnp.bfloat16)
    mats = jnp.einsum("gs,ijs->gij", both, pick, preferred_element_type=jnp.float32)
    mats = mats.astype(jnp.bfloat16)
    return mats[:groups], mats[groups:]


def split_bf16(x):
    hi = lax.reduce_precision(x, exponent_bits=8, mantissa_bits=7)
    lo = x - hi
    return hi.astype(jnp.bfloat16), lo.astype(jnp.bfloat16)


def windows(x, tiles, block, width):
    return jnp.stack([x[k * block : k * block + width] for k in range(tiles)])


def filter_apply(mats, wins, groups, per_group):
    tiles, width, chans = wins.shape
    w4 = wins.reshape(tiles, width, groups, per_group)
    total = None
    for m in mats:
        part = jnp.einsum("gij,kjgc->kigc", m, w4, preferred_element_type=jnp.float32)
        total = part if total is None else total + part
    block = mats[0].shape[1]
    return total.reshape(tiles * block, chans)


def exchange_columns(x, count):
    rows, cols = x.shape
    width = cols // count
    me = lax.axis_index("ctx")
    out = jnp.zeros((count * rows, width), x.dtype)
    own = lax.dynamic_slice_in_dim(x, me * width, width, 1)
    out = lax.dynamic_update_slice_in_dim(out, own, me * rows, 0)
    for shift in range(1, count):
        dest = (me + shift) % count
        chunk = lax.dynamic_slice_in_dim(x, dest * width, width, 1)
        got = lax.ppermute(chunk, "ctx", [(k, (k + shift) % count) for k in range(count)])
        src = (me + count - shift) % count
        out = lax.dynamic_update_slice_in_dim(out, got, src * rows, 0)
    return out


def butterfly_sum(x, axis, count):
    if count & (count - 1):
        return lax.psum(x, axis)
    step = 1
    while step < count:
        x = x + lax.ppermute(x, axis, [(k, k ^ step) for k in range(count)])
        step *= 2
    return x


def butterfly_gather(x, axis, count):
    if count & (count - 1):
        return lax.all_gather(x, axis, axis=0, tiled=True)
    me = lax.axis_index(axis)
    step = 1
    while step < count:
        got = lax.ppermute(x, axis, [(k, k ^ step) for k in range(count)])
        low = (me // step) % 2 == 0
        x = jnp.where(low, jnp.concatenate([x, got]), jnp.concatenate([got, x]))
        step *= 2
    return x


def pair_scatter(partial, count):
    rows = partial.shape[0] // count
    if count % 2:
        return lax.psum_scatter(partial, "ctx", scatter_dimension=0, tiled=True)
    me = lax.axis_index("ctx")
    blocks = partial.reshape(count // 2, 2, rows, partial.shape[1])
    keep = lax.dynamic_index_in_dim(blocks, me % 2, 1, keepdims=False)
    give = lax.dynamic_index_in_dim(blocks, 1 - me % 2, 1, keepdims=False)
    got = lax.ppermute(give, "ctx", [(k, k ^ 1) for k in range(count)])
    summed = (keep + got).reshape(count // 2 * rows, partial.shape[1])
    groups = [[p + 2 * q for q in range(count // 2)] for p in range(2)]
    return lax.psum_scatter(summed, "ctx", scatter_dimension=0, tiled=True, axis_index_groups=groups)


def body(cotangent, out_weight, query_act, key_act, value_act, filters):
    rows, chans = cotangent.shape
    groups, flen = filters.shape
    ctx_count = lax.axis_size("ctx")
    mp_count = lax.axis_size("mp")
    per_group = chans * mp_count // groups
    local_groups = chans // per_group
    halo = flen
    block = 64 if rows % 64 == 0 else rows
    tiles = rows // block
    width = block + halo

    taps = lax.dynamic_slice_in_dim(filters, lax.axis_index("mp") * local_groups, local_groups, 0)
    pad = jnp.zeros((local_groups, width + 1 - flen - 1), jnp.float32)
    one = jnp.zeros((local_groups, 1), jnp.float32)
    seq_causal = jnp.concatenate([one, taps[:, ::-1], pad], 1)
    seq_anti = jnp.concatenate([taps, pad, one], 1)
    zero = lax.axis_index("ctx") // ctx_count
    mats_causal = toeplitz_mats(taps, block, width, halo, True, zero)
    mats_anti = toeplitz_mats(taps, block, width, halo, False, zero)

    cot_rows = lax.all_gather(cotangent, "mp", axis=1, tiled=True)
    cot_rows, mats_causal, mats_anti = lax.optimization_barrier((cot_rows, mats_causal, mats_anti))
    cot_cols = exchange_columns(cot_rows, ctx_count)
    partial = contract(cot_cols, out_weight)
    grad_mixed = pair_scatter(partial, ctx_count)

    fwd = [(k, k + 1) for k in range(ctx_count - 1)]
    bwd = [(k + 1, k) for k in range(ctx_count - 1)]
    product = (key_act.astype(jnp.float32) * value_act.astype(jnp.float32)).astype(jnp.bfloat16)
    prev_tail = lax.ppermute(product[rows - halo :], "ctx", fwd)
    widened = jnp.concatenate([prev_tail, product], 0)
    win_prod = windows(widened, tiles, block, width)
    mixed = filter_apply(mats_causal, win_prod, local_groups, per_group)
    grad_mixed, mixed = lax.optimization_barrier((grad_mixed, mixed))

    grad_conv = (grad_mixed * query_act.astype(jnp.float32)).astype(jnp.bfloat16)
    next_head = lax.ppermute(grad_conv[:halo], "ctx", bwd)
    gc4 = grad_conv.reshape(tiles, block, local_groups, per_group)
    wp4 = win_prod.reshape(tiles, width, local_groups, per_group)
    cross = jnp.einsum("kigc,kjgc->gij", gc4, wp4, preferred_element_type=jnp.float32)
    cross = jnp.pad(cross.reshape(local_groups, block * width), ((0, 0), (0, block)))
    diag = cross.reshape(local_groups, block, width + 1)[:, :, 1 : halo + 1].sum(axis=1)
    scale = (rows * ctx_count * per_group) ** (-0.5)
    diag, next_head = lax.optimization_barrier((diag, next_head))
    local_filters = butterfly_sum(diag[:, ::-1], "ctx", ctx_count) * scale
    grad_filters = butterfly_gather(local_filters, "mp", mp_count)
    trailing = jnp.concatenate([grad_conv, next_head], 0)
    win_grad = windows(trailing, tiles, block, width)
    grad_product = filter_apply(mats_anti, win_grad, local_groups, per_group)
    grad_filters, grad_product = lax.optimization_barrier((grad_filters, grad_product))


    grad_query = (grad_mixed * mixed).astype(jnp.bfloat16)
    grad_key = (grad_product * value_act.astype(jnp.float32)).astype(jnp.bfloat16)
    grad_value = (grad_product * key_act.astype(jnp.float32)).astype(jnp.bfloat16)
    return (grad_query, grad_key, grad_value, grad_filters)


def solution(mesh):
    in_specs = (P("ctx", "mp"), P("mp", "ctx"), P("ctx", "mp"), P("ctx", "mp"), P("ctx", "mp"), P())
    out_specs = (P("ctx", "mp"), P("ctx", "mp"), P("ctx", "mp"), P())
    return jax.shard_map(body, mesh=mesh, in_specs=in_specs, out_specs=out_specs, check_vma=False)
```

```python
import jax
import jax.numpy as jnp
from jax import lax
from jax.sharding import PartitionSpec as P


def contract(left, right):
    return lax.dot_general(
        left, right, (((1,), (1,)), ((), ())), preferred_element_type=jnp.float32
    )


def toeplitz(seq, block, width):
    groups = seq.shape[0]
    flat = jnp.tile(seq, (1, block))[:, : block * width]
    return flat.reshape(groups, block, width)


def toeplitz_mats(taps, block, width, halo, causal, zero):
    groups, flen = taps.shape
    hi = lax.reduce_precision(taps, exponent_bits=8, mantissa_bits=7)
    both = jnp.concatenate([hi, taps - hi], 0).astype(jnp.bfloat16)
    i = lax.broadcasted_iota(jnp.int32, (block, width, flen), 0)
    j = lax.broadcasted_iota(jnp.int32, (block, width, flen), 1)
    s = lax.broadcasted_iota(jnp.int32, (block, width, flen), 2) + zero
    lag = i + halo - j if causal else j - i
    pick = (lag == s).astype(jnp.bfloat16)
    mats = jnp.einsum("gs,ijs->gij", both, pick, preferred_element_type=jnp.float32)
    mats = mats.astype(jnp.bfloat16)
    return mats[:groups], mats[groups:]


def split_bf16(x):
    hi = lax.reduce_precision(x, exponent_bits=8, mantissa_bits=7)
    lo = x - hi
    return hi.astype(jnp.bfloat16), lo.astype(jnp.bfloat16)


def windows(x, tiles, block, width):
    return jnp.stack([x[k * block : k * block + width] for k in range(tiles)])


def filter_apply(mats, wins, groups, per_group):
    tiles, width, chans = wins.shape
    w4 = wins.reshape(tiles, width, groups, per_group)
    total = None
    for m in mats:
        part = jnp.einsum("gij,kjgc->kigc", m, w4, preferred_element_type=jnp.float32)
        total = part if total is None else total + part
    block = mats[0].shape[1]
    return total.reshape(tiles * block, chans)


def exchange_columns(x, count):
    rows, cols = x.shape
    width = cols // count
    me = lax.axis_index("ctx")
    out = jnp.zeros((count * rows, width), x.dtype)
    own = lax.dynamic_slice_in_dim(x, me * width, width, 1)
    out = lax.dynamic_update_slice_in_dim(out, own, me * rows, 0)
    for shift in range(1, count):
        dest = (me + shift) % count
        chunk = lax.dynamic_slice_in_dim(x, dest * width, width, 1)
        got = lax.ppermute(chunk, "ctx", [(k, (k + shift) % count) for k in range(count)])
        src = (me + count - shift) % count
        out = lax.dynamic_update_slice_in_dim(out, got, src * rows, 0)
    return out


def butterfly_sum(x, axis, count):
    if count & (count - 1):
        return lax.psum(x, axis)
    step = 1
    while step < count:
        x = x + lax.ppermute(x, axis, [(k, k ^ step) for k in range(count)])
        step *= 2
    return x


def butterfly_gather(x, axis, count):
    if count & (count - 1):
        return lax.all_gather(x, axis, axis=0, tiled=True)
    me = lax.axis_index(axis)
    step = 1
    while step < count:
        got = lax.ppermute(x, axis, [(k, k ^ step) for k in range(count)])
        low = (me // step) % 2 == 0
        x = jnp.where(low, jnp.concatenate([x, got]), jnp.concatenate([got, x]))
        step *= 2
    return x


def body(cotangent, out_weight, query_act, key_act, value_act, filters):
    rows, chans = cotangent.shape
    groups, flen = filters.shape
    ctx_count = lax.axis_size("ctx")
    mp_count = lax.axis_size("mp")
    per_group = chans * mp_count // groups
    local_groups = chans // per_group
    halo = flen
    block = 64 if rows % 64 == 0 else rows
    tiles = rows // block
    width = block + halo

    taps = lax.dynamic_slice_in_dim(filters, lax.axis_index("mp") * local_groups, local_groups, 0)
    pad = jnp.zeros((local_groups, width + 1 - flen - 1), jnp.float32)
    one = jnp.zeros((local_groups, 1), jnp.float32)
    seq_causal = jnp.concatenate([one, taps[:, ::-1], pad], 1)
    seq_anti = jnp.concatenate([taps, pad, one], 1)
    zero = lax.axis_index("ctx") // ctx_count
    mats_causal = toeplitz_mats(taps, block, width, halo, True, zero)
    mats_anti = toeplitz_mats(taps, block, width, halo, False, zero)

    cot_rows = lax.all_gather(cotangent, "mp", axis=1, tiled=True)
    cot_rows, mats_causal, mats_anti = lax.optimization_barrier((cot_rows, mats_causal, mats_anti))
    cot_cols = exchange_columns(cot_rows, ctx_count)
    partial = contract(cot_cols, out_weight)
    grad_mixed = lax.psum_scatter(partial, "ctx", scatter_dimension=0, tiled=True)

    fwd = [(k, k + 1) for k in range(ctx_count - 1)]
    bwd = [(k + 1, k) for k in range(ctx_count - 1)]
    product = (key_act.astype(jnp.float32) * value_act.astype(jnp.float32)).astype(jnp.bfloat16)
    prev_tail = lax.ppermute(product[rows - halo :], "ctx", fwd)
    widened = jnp.concatenate([prev_tail, product], 0)
    win_prod = windows(widened, tiles, block, width)
    mixed = filter_apply(mats_causal, win_prod, local_groups, per_group)
    grad_mixed, mixed = lax.optimization_barrier((grad_mixed, mixed))

    grad_conv = (grad_mixed * query_act.astype(jnp.float32)).astype(jnp.bfloat16)
    next_head = lax.ppermute(grad_conv[:halo], "ctx", bwd)
    gc4 = grad_conv.reshape(tiles, block, local_groups, per_group)
    wp4 = win_prod.reshape(tiles, width, local_groups, per_group)
    cross = jnp.einsum("kigc,kjgc->gij", gc4, wp4, preferred_element_type=jnp.float32)
    i = lax.broadcasted_iota(jnp.int32, (block, width, flen), 0)
    j = lax.broadcasted_iota(jnp.int32, (block, width, flen), 1)
    lag = lax.broadcasted_iota(jnp.int32, (block, width, flen), 2) + zero
    pick = (i + halo - j == lag).astype(jnp.bfloat16)
    cross_hi = lax.reduce_precision(cross, exponent_bits=8, mantissa_bits=7)
    diag = None
    for piece in (cross_hi, cross - cross_hi):
        term = jnp.einsum("gij,ijs->gs", piece.astype(jnp.bfloat16), pick, preferred_element_type=jnp.float32)
        diag = term if diag is None else diag + term
    scale = (rows * ctx_count * per_group) ** (-0.5)
    diag, next_head = lax.optimization_barrier((diag, next_head))
    local_filters = butterfly_sum(diag, "ctx", ctx_count) * scale
    grad_filters = butterfly_gather(local_filters, "mp", mp_count)
    trailing = jnp.concatenate([grad_conv, next_head], 0)
    win_grad = windows(trailing, tiles, block, width)
    grad_product = filter_apply(mats_anti, win_grad, local_groups, per_group)
    grad_filters, grad_product = lax.optimization_barrier((grad_filters, grad_product))


    grad_query = (grad_mixed * mixed).astype(jnp.bfloat16)
    grad_key = (grad_product * value_act.astype(jnp.float32)).astype(jnp.bfloat16)
    grad_value = (grad_product * key_act.astype(jnp.float32)).astype(jnp.bfloat16)
    return (grad_query, grad_key, grad_value, grad_filters)


def solution(mesh):
    in_specs = (P("ctx", "mp"), P("mp", "ctx"), P("ctx", "mp"), P("ctx", "mp"), P("ctx", "mp"), P())
    out_specs = (P("ctx", "mp"), P("ctx", "mp"), P("ctx", "mp"), P())
    return jax.shard_map(body, mesh=mesh, in_specs=in_specs, out_specs=out_specs, check_vma=False)
```

```python
import jax
import jax.numpy as jnp
from jax import lax
from jax.sharding import PartitionSpec as P


def contract(left, right):
    return lax.dot_general(
        left, right, (((1,), (1,)), ((), ())), preferred_element_type=jnp.float32
    )


def toeplitz(seq, block, width):
    groups = seq.shape[0]
    flat = jnp.tile(seq, (1, block))[:, : block * width]
    return flat.reshape(groups, block, width)


def toeplitz_mats(taps, block, width, halo, causal, zero):
    groups, flen = taps.shape
    hi = lax.reduce_precision(taps, exponent_bits=8, mantissa_bits=7)
    both = jnp.concatenate([hi, taps - hi], 0).astype(jnp.bfloat16)
    i = lax.broadcasted_iota(jnp.int32, (block, width, flen), 0)
    j = lax.broadcasted_iota(jnp.int32, (block, width, flen), 1)
    s = lax.broadcasted_iota(jnp.int32, (block, width, flen), 2) + zero
    lag = i + halo - j if causal else j - i
    pick = (lag == s).astype(jnp.bfloat16)
    mats = jnp.einsum("gs,ijs->gij", both, pick, preferred_element_type=jnp.float32)
    mats = mats.astype(jnp.bfloat16)
    return mats[:groups], mats[groups:]


def split_bf16(x):
    hi = lax.reduce_precision(x, exponent_bits=8, mantissa_bits=7)
    lo = x - hi
    return hi.astype(jnp.bfloat16), lo.astype(jnp.bfloat16)


def windows(x, tiles, block, width):
    return jnp.stack([x[k * block : k * block + width] for k in range(tiles)])


def filter_apply(mats, wins, groups, per_group):
    tiles, width, chans = wins.shape
    w4 = wins.reshape(tiles, width, groups, per_group)
    total = None
    for m in mats:
        part = jnp.einsum("gij,kjgc->kigc", m, w4, preferred_element_type=jnp.float32)
        total = part if total is None else total + part
    block = mats[0].shape[1]
    return total.reshape(tiles * block, chans)


def exchange_columns(x, count):
    rows, cols = x.shape
    width = cols // count
    me = lax.axis_index("ctx")
    out = jnp.zeros((count * rows, width), x.dtype)
    own = lax.dynamic_slice_in_dim(x, me * width, width, 1)
    out = lax.dynamic_update_slice_in_dim(out, own, me * rows, 0)
    for shift in range(1, count):
        dest = (me + shift) % count
        chunk = lax.dynamic_slice_in_dim(x, dest * width, width, 1)
        got = lax.ppermute(chunk, "ctx", [(k, (k + shift) % count) for k in range(count)])
        src = (me + count - shift) % count
        out = lax.dynamic_update_slice_in_dim(out, got, src * rows, 0)
    return out


def butterfly_sum(x, axis, count):
    if count & (count - 1):
        return lax.psum(x, axis)
    step = 1
    while step < count:
        x = x + lax.ppermute(x, axis, [(k, k ^ step) for k in range(count)])
        step *= 2
    return x


def butterfly_gather(x, axis, count):
    if count & (count - 1):
        return lax.all_gather(x, axis, axis=0, tiled=True)
    me = lax.axis_index(axis)
    step = 1
    while step < count:
        got = lax.ppermute(x, axis, [(k, k ^ step) for k in range(count)])
        low = (me // step) % 2 == 0
        x = jnp.where(low, jnp.concatenate([x, got]), jnp.concatenate([got, x]))
        step *= 2
    return x


def scatter_sum(partial, count):
    rows = partial.shape[0] // count
    me = lax.axis_index("ctx")
    acc = lax.dynamic_slice_in_dim(partial, me * rows, rows, 0)
    for shift in range(1, count):
        dest = (me + shift) % count
        chunk = lax.dynamic_slice_in_dim(partial, dest * rows, rows, 0)
        acc = acc + lax.ppermute(chunk, "ctx", [(k, (k + shift) % count) for k in range(count)])
    return acc


def body(cotangent, out_weight, query_act, key_act, value_act, filters):
    rows, chans = cotangent.shape
    groups, flen = filters.shape
    ctx_count = lax.axis_size("ctx")
    mp_count = lax.axis_size("mp")
    per_group = chans * mp_count // groups
    local_groups = chans // per_group
    halo = flen
    block = 64 if rows % 64 == 0 else rows
    tiles = rows // block
    width = block + halo

    taps = lax.dynamic_slice_in_dim(filters, lax.axis_index("mp") * local_groups, local_groups, 0)
    pad = jnp.zeros((local_groups, width + 1 - flen - 1), jnp.float32)
    one = jnp.zeros((local_groups, 1), jnp.float32)
    seq_causal = jnp.concatenate([one, taps[:, ::-1], pad], 1)
    seq_anti = jnp.concatenate([taps, pad, one], 1)
    zero = lax.axis_index("ctx") // ctx_count
    mats_causal = toeplitz_mats(taps, block, width, halo, True, zero)
    mats_anti = toeplitz_mats(taps, block, width, halo, False, zero)

    cot_rows = lax.all_gather(cotangent, "mp", axis=1, tiled=True)
    cot_rows, mats_causal, mats_anti = lax.optimization_barrier((cot_rows, mats_causal, mats_anti))
    cot_cols = exchange_columns(cot_rows, ctx_count)
    partial = contract(cot_cols, out_weight)
    half = chans // 2
    grad_mixed = jnp.concatenate(
        [
            lax.psum_scatter(partial[:, :half], "ctx", scatter_dimension=0, tiled=True),
            scatter_sum(partial[:, half:], ctx_count),
        ],
        1,
    )

    fwd = [(k, k + 1) for k in range(ctx_count - 1)]
    bwd = [(k + 1, k) for k in range(ctx_count - 1)]
    product = (key_act.astype(jnp.float32) * value_act.astype(jnp.float32)).astype(jnp.bfloat16)
    prev_tail = lax.ppermute(product[rows - halo :], "ctx", fwd)
    widened = jnp.concatenate([prev_tail, product], 0)
    win_prod = windows(widened, tiles, block, width)
    mixed = filter_apply(mats_causal, win_prod, local_groups, per_group)
    grad_mixed, mixed = lax.optimization_barrier((grad_mixed, mixed))

    grad_conv = (grad_mixed * query_act.astype(jnp.float32)).astype(jnp.bfloat16)
    next_head = lax.ppermute(grad_conv[:halo], "ctx", bwd)
    gc4 = grad_conv.reshape(tiles, block, local_groups, per_group)
    wp4 = win_prod.reshape(tiles, width, local_groups, per_group)
    cross = jnp.einsum("kigc,kjgc->gij", gc4, wp4, preferred_element_type=jnp.float32)
    i = lax.broadcasted_iota(jnp.int32, (block, width, flen), 0)
    j = lax.broadcasted_iota(jnp.int32, (block, width, flen), 1)
    lag = lax.broadcasted_iota(jnp.int32, (block, width, flen), 2) + zero
    pick = (i + halo - j == lag).astype(jnp.bfloat16)
    cross_hi = lax.reduce_precision(cross, exponent_bits=8, mantissa_bits=7)
    diag = None
    for piece in (cross_hi, cross - cross_hi):
        term = jnp.einsum("gij,ijs->gs", piece.astype(jnp.bfloat16), pick, preferred_element_type=jnp.float32)
        diag = term if diag is None else diag + term
    scale = (rows * ctx_count * per_group) ** (-0.5)
    diag, next_head = lax.optimization_barrier((diag, next_head))
    local_filters = butterfly_sum(diag, "ctx", ctx_count) * scale
    grad_filters = butterfly_gather(local_filters, "mp", mp_count)
    trailing = jnp.concatenate([grad_conv, next_head], 0)
    win_grad = windows(trailing, tiles, block, width)
    grad_product = filter_apply(mats_anti, win_grad, local_groups, per_group)
    grad_filters, grad_product = lax.optimization_barrier((grad_filters, grad_product))


    grad_query = (grad_mixed * mixed).astype(jnp.bfloat16)
    grad_key = (grad_product * value_act.astype(jnp.float32)).astype(jnp.bfloat16)
    grad_value = (grad_product * key_act.astype(jnp.float32)).astype(jnp.bfloat16)
    return (grad_query, grad_key, grad_value, grad_filters)


def solution(mesh):
    in_specs = (P("ctx", "mp"), P("mp", "ctx"), P("ctx", "mp"), P("ctx", "mp"), P("ctx", "mp"), P())
    out_specs = (P("ctx", "mp"), P("ctx", "mp"), P("ctx", "mp"), P())
    return jax.shard_map(body, mesh=mesh, in_specs=in_specs, out_specs=out_specs, check_vma=False)
```

```python
import jax
import jax.numpy as jnp
from jax import lax
from jax.sharding import PartitionSpec as P


def contract(left, right):
    return lax.dot_general(
        left, right, (((1,), (1,)), ((), ())), preferred_element_type=jnp.float32
    )


def toeplitz(seq, block, width):
    groups = seq.shape[0]
    flat = jnp.tile(seq, (1, block))[:, : block * width]
    return flat.reshape(groups, block, width)


def toeplitz_mats(taps, block, width, halo, causal, zero):
    groups, flen = taps.shape
    hi = lax.reduce_precision(taps, exponent_bits=8, mantissa_bits=7)
    both = jnp.concatenate([hi, taps - hi], 0).astype(jnp.bfloat16)
    i = lax.broadcasted_iota(jnp.int32, (block, width, flen), 0)
    j = lax.broadcasted_iota(jnp.int32, (block, width, flen), 1)
    s = lax.broadcasted_iota(jnp.int32, (block, width, flen), 2) + zero
    lag = i + halo - j if causal else j - i
    pick = (lag == s).astype(jnp.bfloat16)
    mats = jnp.einsum("gs,ijs->gij", both, pick, preferred_element_type=jnp.float32)
    mats = mats.astype(jnp.bfloat16)
    return mats[:groups], mats[groups:]


def split_bf16(x):
    hi = lax.reduce_precision(x, exponent_bits=8, mantissa_bits=7)
    lo = x - hi
    return hi.astype(jnp.bfloat16), lo.astype(jnp.bfloat16)


def windows(x, tiles, block, width):
    return jnp.stack([x[k * block : k * block + width] for k in range(tiles)])


def filter_apply(mat, wins, groups, per_group):
    tiles, width, chans = wins.shape
    w4 = jnp.concatenate([wins, wins], 1).reshape(tiles, 2 * width, groups, per_group)
    total = jnp.einsum("gij,kjgc->kigc", mat, w4, preferred_element_type=jnp.float32)
    return total.reshape(tiles * mat.shape[1], chans)


def exchange_columns(x, count):
    rows, cols = x.shape
    width = cols // count
    me = lax.axis_index("ctx")
    out = jnp.zeros((count * rows, width), x.dtype)
    own = lax.dynamic_slice_in_dim(x, me * width, width, 1)
    out = lax.dynamic_update_slice_in_dim(out, own, me * rows, 0)
    for shift in range(1, count):
        dest = (me + shift) % count
        chunk = lax.dynamic_slice_in_dim(x, dest * width, width, 1)
        got = lax.ppermute(chunk, "ctx", [(k, (k + shift) % count) for k in range(count)])
        src = (me + count - shift) % count
        out = lax.dynamic_update_slice_in_dim(out, got, src * rows, 0)
    return out


def butterfly_sum(x, axis, count):
    if count & (count - 1):
        return lax.psum(x, axis)
    step = 1
    while step < count:
        x = x + lax.ppermute(x, axis, [(k, k ^ step) for k in range(count)])
        step *= 2
    return x


def butterfly_gather(x, axis, count):
    if count & (count - 1):
        return lax.all_gather(x, axis, axis=0, tiled=True)
    me = lax.axis_index(axis)
    step = 1
    while step < count:
        got = lax.ppermute(x, axis, [(k, k ^ step) for k in range(count)])
        low = (me // step) % 2 == 0
        x = jnp.where(low, jnp.concatenate([x, got]), jnp.concatenate([got, x]))
        step *= 2
    return x


def body(cotangent, out_weight, query_act, key_act, value_act, filters):
    rows, chans = cotangent.shape
    groups, flen = filters.shape
    ctx_count = lax.axis_size("ctx")
    mp_count = lax.axis_size("mp")
    per_group = chans * mp_count // groups
    local_groups = chans // per_group
    halo = flen
    block = 64 if rows % 64 == 0 else rows
    tiles = rows // block
    width = block + halo

    taps = lax.dynamic_slice_in_dim(filters, lax.axis_index("mp") * local_groups, local_groups, 0)
    pad = jnp.zeros((local_groups, width + 1 - flen - 1), jnp.float32)
    one = jnp.zeros((local_groups, 1), jnp.float32)
    seq_causal = jnp.concatenate([one, taps[:, ::-1], pad], 1)
    seq_anti = jnp.concatenate([taps, pad, one], 1)
    zero = lax.axis_index("ctx") // ctx_count
    mats_causal = toeplitz_mats(taps, block, width, halo, True, zero)
    mats_anti = toeplitz_mats(taps, block, width, halo, False, zero)

    cot_rows = lax.all_gather(cotangent, "mp", axis=1, tiled=True)
    mats_causal = jnp.concatenate(mats_causal, 2)
    mats_anti = jnp.concatenate(mats_anti, 2)
    cot_rows, mats_causal, mats_anti = lax.optimization_barrier((cot_rows, mats_causal, mats_anti))
    cot_cols = exchange_columns(cot_rows, ctx_count)
    partial = contract(cot_cols, out_weight)
    grad_mixed = lax.psum_scatter(partial, "ctx", scatter_dimension=0, tiled=True)

    fwd = [(k, k + 1) for k in range(ctx_count - 1)]
    bwd = [(k + 1, k) for k in range(ctx_count - 1)]
    product = (key_act.astype(jnp.float32) * value_act.astype(jnp.float32)).astype(jnp.bfloat16)
    prev_tail = lax.ppermute(product[rows - halo :], "ctx", fwd)
    widened = jnp.concatenate([prev_tail, product], 0)
    win_prod = windows(widened, tiles, block, width)
    mixed = filter_apply(mats_causal, win_prod, local_groups, per_group)
    grad_mixed, mixed = lax.optimization_barrier((grad_mixed, mixed))

    grad_conv = (grad_mixed * query_act.astype(jnp.float32)).astype(jnp.bfloat16)
    next_head = lax.ppermute(grad_conv[:halo], "ctx", bwd)
    gc4 = grad_conv.reshape(tiles, block, local_groups, per_group)
    wp4 = win_prod.reshape(tiles, width, local_groups, per_group)
    cross = jnp.einsum("kigc,kjgc->gij", gc4, wp4, preferred_element_type=jnp.float32)
    i = lax.broadcasted_iota(jnp.int32, (block, width, flen), 0)
    j = lax.broadcasted_iota(jnp.int32, (block, width, flen), 1)
    lag = lax.broadcasted_iota(jnp.int32, (block, width, flen), 2) + zero
    pick = (i + halo - j == lag).astype(jnp.bfloat16)
    cross_hi = lax.reduce_precision(cross, exponent_bits=8, mantissa_bits=7)
    diag = None
    for piece in (cross_hi, cross - cross_hi):
        term = jnp.einsum("gij,ijs->gs", piece.astype(jnp.bfloat16), pick, preferred_element_type=jnp.float32)
        diag = term if diag is None else diag + term
    scale = (rows * ctx_count * per_group) ** (-0.5)
    diag, next_head = lax.optimization_barrier((diag, next_head))
    local_filters = butterfly_sum(diag, "ctx", ctx_count) * scale
    grad_filters = butterfly_gather(local_filters, "mp", mp_count)
    trailing = jnp.concatenate([grad_conv, next_head], 0)
    win_grad = windows(trailing, tiles, block, width)
    grad_product = filter_apply(mats_anti, win_grad, local_groups, per_group)
    grad_filters, grad_product = lax.optimization_barrier((grad_filters, grad_product))


    grad_query = (grad_mixed * mixed).astype(jnp.bfloat16)
    grad_key = (grad_product * value_act.astype(jnp.float32)).astype(jnp.bfloat16)
    grad_value = (grad_product * key_act.astype(jnp.float32)).astype(jnp.bfloat16)
    return (grad_query, grad_key, grad_value, grad_filters)


def solution(mesh):
    in_specs = (P("ctx", "mp"), P("mp", "ctx"), P("ctx", "mp"), P("ctx", "mp"), P("ctx", "mp"), P())
    out_specs = (P("ctx", "mp"), P("ctx", "mp"), P("ctx", "mp"), P())
    return jax.shard_map(body, mesh=mesh, in_specs=in_specs, out_specs=out_specs, check_vma=False)
```

```python
import jax
import jax.numpy as jnp
from jax import lax
from jax.sharding import PartitionSpec as P


def contract(left, right):
    return lax.dot_general(
        left, right, (((1,), (1,)), ((), ())), preferred_element_type=jnp.float32
    )


def toeplitz(seq, block, width):
    groups = seq.shape[0]
    flat = jnp.tile(seq, (1, block))[:, : block * width]
    return flat.reshape(groups, block, width)


def toeplitz_mats(taps, block, width, halo, causal, zero):
    groups, flen = taps.shape
    hi = lax.reduce_precision(taps, exponent_bits=8, mantissa_bits=7)
    both = jnp.concatenate([hi, taps - hi], 0).astype(jnp.bfloat16)
    i = lax.broadcasted_iota(jnp.int32, (block, width, flen), 0)
    j = lax.broadcasted_iota(jnp.int32, (block, width, flen), 1)
    s = lax.broadcasted_iota(jnp.int32, (block, width, flen), 2) + zero
    lag = i + halo - j if causal else j - i
    pick = (lag == s).astype(jnp.bfloat16)
    mats = jnp.einsum("gs,ijs->gij", both, pick, preferred_element_type=jnp.float32)
    mats = mats.astype(jnp.bfloat16)
    return mats[:groups], mats[groups:]


def split_bf16(x):
    hi = lax.reduce_precision(x, exponent_bits=8, mantissa_bits=7)
    lo = x - hi
    return hi.astype(jnp.bfloat16), lo.astype(jnp.bfloat16)


def windows(x, tiles, block, width):
    return jnp.stack([x[k * block : k * block + width] for k in range(tiles)])


def filter_apply(mats, wins, groups, per_group):
    tiles, width, chans = wins.shape
    w4 = wins.reshape(tiles, width, groups, per_group)
    total = None
    for m in mats:
        part = jnp.einsum("gij,kjgc->kigc", m, w4, preferred_element_type=jnp.float32)
        total = part if total is None else total + part
    block = mats[0].shape[1]
    return total.reshape(tiles * block, chans)


def exchange_columns(x, count):
    rows, cols = x.shape
    width = cols // count
    me = lax.axis_index("ctx")
    out = jnp.zeros((count * rows, width), x.dtype)
    own = lax.dynamic_slice_in_dim(x, me * width, width, 1)
    out = lax.dynamic_update_slice_in_dim(out, own, me * rows, 0)
    for shift in range(1, count):
        dest = (me + shift) % count
        chunk = lax.dynamic_slice_in_dim(x, dest * width, width, 1)
        got = lax.ppermute(chunk, "ctx", [(k, (k + shift) % count) for k in range(count)])
        src = (me + count - shift) % count
        out = lax.dynamic_update_slice_in_dim(out, got, src * rows, 0)
    return out


def butterfly_sum(x, axis, count):
    if count & (count - 1):
        return lax.psum(x, axis)
    step = 1
    while step < count:
        x = x + lax.ppermute(x, axis, [(k, k ^ step) for k in range(count)])
        step *= 2
    return x


def butterfly_gather(x, axis, count):
    if count & (count - 1):
        return lax.all_gather(x, axis, axis=0, tiled=True)
    me = lax.axis_index(axis)
    step = 1
    while step < count:
        got = lax.ppermute(x, axis, [(k, k ^ step) for k in range(count)])
        low = (me // step) % 2 == 0
        x = jnp.where(low, jnp.concatenate([x, got]), jnp.concatenate([got, x]))
        step *= 2
    return x


def body(cotangent, out_weight, query_act, key_act, value_act, filters):
    rows, chans = cotangent.shape
    groups, flen = filters.shape
    ctx_count = lax.axis_size("ctx")
    mp_count = lax.axis_size("mp")
    per_group = chans * mp_count // groups
    local_groups = chans // per_group
    halo = flen
    block = 32 if rows % 32 == 0 else rows
    tiles = rows // block
    width = block + halo

    taps = lax.dynamic_slice_in_dim(filters, lax.axis_index("mp") * local_groups, local_groups, 0)
    pad = jnp.zeros((local_groups, width + 1 - flen - 1), jnp.float32)
    one = jnp.zeros((local_groups, 1), jnp.float32)
    seq_causal = jnp.concatenate([one, taps[:, ::-1], pad], 1)
    seq_anti = jnp.concatenate([taps, pad, one], 1)
    zero = lax.axis_index("ctx") // ctx_count
    mats_causal = toeplitz_mats(taps, block, width, halo, True, zero)
    mats_anti = toeplitz_mats(taps, block, width, halo, False, zero)

    cot_rows = lax.all_gather(cotangent, "mp", axis=1, tiled=True)
    cot_rows, mats_causal, mats_anti = lax.optimization_barrier((cot_rows, mats_causal, mats_anti))
    cot_cols = exchange_columns(cot_rows, ctx_count)
    partial = contract(cot_cols, out_weight)
    grad_mixed = lax.psum_scatter(partial, "ctx", scatter_dimension=0, tiled=True)

    fwd = [(k, k + 1) for k in range(ctx_count - 1)]
    bwd = [(k + 1, k) for k in range(ctx_count - 1)]
    product = (key_act.astype(jnp.float32) * value_act.astype(jnp.float32)).astype(jnp.bfloat16)
    prev_tail = lax.ppermute(product[rows - halo :], "ctx", fwd)
    widened = jnp.concatenate([prev_tail, product], 0)
    win_prod = windows(widened, tiles, block, width)
    mixed = filter_apply(mats_causal, win_prod, local_groups, per_group)
    grad_mixed, mixed = lax.optimization_barrier((grad_mixed, mixed))

    grad_conv = (grad_mixed * query_act.astype(jnp.float32)).astype(jnp.bfloat16)
    next_head = lax.ppermute(grad_conv[:halo], "ctx", bwd)
    gc4 = grad_conv.reshape(tiles, block, local_groups, per_group)
    wp4 = win_prod.reshape(tiles, width, local_groups, per_group)
    cross = jnp.einsum("kigc,kjgc->gij", gc4, wp4, preferred_element_type=jnp.float32)
    i = lax.broadcasted_iota(jnp.int32, (block, width, flen), 0)
    j = lax.broadcasted_iota(jnp.int32, (block, width, flen), 1)
    lag = lax.broadcasted_iota(jnp.int32, (block, width, flen), 2) + zero
    pick = (i + halo - j == lag).astype(jnp.bfloat16)
    cross_hi = lax.reduce_precision(cross, exponent_bits=8, mantissa_bits=7)
    diag = None
    for piece in (cross_hi, cross - cross_hi):
        term = jnp.einsum("gij,ijs->gs", piece.astype(jnp.bfloat16), pick, preferred_element_type=jnp.float32)
        diag = term if diag is None else diag + term
    scale = (rows * ctx_count * per_group) ** (-0.5)
    diag, next_head = lax.optimization_barrier((diag, next_head))
    local_filters = butterfly_sum(diag, "ctx", ctx_count) * scale
    grad_filters = butterfly_gather(local_filters, "mp", mp_count)
    trailing = jnp.concatenate([grad_conv, next_head], 0)
    win_grad = windows(trailing, tiles, block, width)
    grad_product = filter_apply(mats_anti, win_grad, local_groups, per_group)
    grad_filters, grad_product = lax.optimization_barrier((grad_filters, grad_product))


    grad_query = (grad_mixed * mixed).astype(jnp.bfloat16)
    grad_key = (grad_product * value_act.astype(jnp.float32)).astype(jnp.bfloat16)
    grad_value = (grad_product * key_act.astype(jnp.float32)).astype(jnp.bfloat16)
    return (grad_query, grad_key, grad_value, grad_filters)


def solution(mesh):
    in_specs = (P("ctx", "mp"), P("mp", "ctx"), P("ctx", "mp"), P("ctx", "mp"), P("ctx", "mp"), P())
    out_specs = (P("ctx", "mp"), P("ctx", "mp"), P("ctx", "mp"), P())
    return jax.shard_map(body, mesh=mesh, in_specs=in_specs, out_specs=out_specs, check_vma=False)
```

```python
import jax
import jax.numpy as jnp
from jax import lax
from jax.sharding import PartitionSpec as P


def contract(left, right):
    return lax.dot_general(
        left, right, (((1,), (1,)), ((), ())), preferred_element_type=jnp.float32
    )


def toeplitz(seq, block, width):
    groups = seq.shape[0]
    flat = jnp.tile(seq, (1, block))[:, : block * width]
    return flat.reshape(groups, block, width)


def toeplitz_mats(taps, block, width, halo, causal, zero):
    groups, flen = taps.shape
    hi = lax.reduce_precision(taps, exponent_bits=8, mantissa_bits=7)
    both = jnp.concatenate([hi, taps - hi], 0).astype(jnp.bfloat16)
    i = lax.broadcasted_iota(jnp.int32, (block, width, flen), 0)
    j = lax.broadcasted_iota(jnp.int32, (block, width, flen), 1)
    s = lax.broadcasted_iota(jnp.int32, (block, width, flen), 2) + zero
    lag = i + halo - j if causal else j - i
    pick = (lag == s).astype(jnp.bfloat16)
    mats = jnp.einsum("gs,ijs->gij", both, pick, preferred_element_type=jnp.float32)
    mats = mats.astype(jnp.bfloat16)
    return mats[:groups], mats[groups:]


def split_bf16(x):
    hi = lax.reduce_precision(x, exponent_bits=8, mantissa_bits=7)
    lo = x - hi
    return hi.astype(jnp.bfloat16), lo.astype(jnp.bfloat16)


def windows(x, tiles, block, width):
    return jnp.stack([x[k * block : k * block + width] for k in range(tiles)])


def filter_apply(mats, wins, groups, per_group):
    tiles, width, chans = wins.shape
    w4 = wins.reshape(tiles, width, groups, per_group)
    total = None
    for m in mats:
        part = jnp.einsum("gij,kjgc->kigc", m, w4, preferred_element_type=jnp.float32)
        total = part if total is None else total + part
    block = mats[0].shape[1]
    return total.reshape(tiles * block, chans)


def exchange_columns(x, count):
    rows, cols = x.shape
    width = cols // count
    me = lax.axis_index("ctx")
    out = jnp.zeros((count * rows, width), x.dtype)
    own = lax.dynamic_slice_in_dim(x, me * width, width, 1)
    out = lax.dynamic_update_slice_in_dim(out, own, me * rows, 0)
    for shift in range(1, count):
        dest = (me + shift) % count
        chunk = lax.dynamic_slice_in_dim(x, dest * width, width, 1)
        got = lax.ppermute(chunk, "ctx", [(k, (k + shift) % count) for k in range(count)])
        src = (me + count - shift) % count
        out = lax.dynamic_update_slice_in_dim(out, got, src * rows, 0)
    return out


def exchange_contract(x, weight, count):
    rows, cols = x.shape
    width = cols // count
    me = lax.axis_index("ctx")
    out = jnp.zeros((count * rows, weight.shape[0]), jnp.float32)
    own = lax.dynamic_slice_in_dim(x, me * width, width, 1)
    out = lax.dynamic_update_slice_in_dim(out, contract(own, weight), me * rows, 0)
    for shift in range(1, count):
        dest = (me + shift) % count
        chunk = lax.dynamic_slice_in_dim(x, dest * width, width, 1)
        got = lax.ppermute(chunk, "ctx", [(k, (k + shift) % count) for k in range(count)])
        src = (me + count - shift) % count
        out = lax.dynamic_update_slice_in_dim(out, contract(got, weight), src * rows, 0)
    return out


def butterfly_sum(x, axis, count):
    if count & (count - 1):
        return lax.psum(x, axis)
    step = 1
    while step < count:
        x = x + lax.ppermute(x, axis, [(k, k ^ step) for k in range(count)])
        step *= 2
    return x


def butterfly_gather(x, axis, count):
    if count & (count - 1):
        return lax.all_gather(x, axis, axis=0, tiled=True)
    me = lax.axis_index(axis)
    step = 1
    while step < count:
        got = lax.ppermute(x, axis, [(k, k ^ step) for k in range(count)])
        low = (me // step) % 2 == 0
        x = jnp.where(low, jnp.concatenate([x, got]), jnp.concatenate([got, x]))
        step *= 2
    return x


def body(cotangent, out_weight, query_act, key_act, value_act, filters):
    rows, chans = cotangent.shape
    groups, flen = filters.shape
    ctx_count = lax.axis_size("ctx")
    mp_count = lax.axis_size("mp")
    per_group = chans * mp_count // groups
    local_groups = chans // per_group
    halo = flen
    block = 64 if rows % 64 == 0 else rows
    tiles = rows // block
    width = block + halo

    taps = lax.dynamic_slice_in_dim(filters, lax.axis_index("mp") * local_groups, local_groups, 0)
    pad = jnp.zeros((local_groups, width + 1 - flen - 1), jnp.float32)
    one = jnp.zeros((local_groups, 1), jnp.float32)
    seq_causal = jnp.concatenate([one, taps[:, ::-1], pad], 1)
    seq_anti = jnp.concatenate([taps, pad, one], 1)
    zero = lax.axis_index("ctx") // ctx_count
    mats_causal = toeplitz_mats(taps, block, width, halo, True, zero)
    mats_anti = toeplitz_mats(taps, block, width, halo, False, zero)

    cot_rows = lax.all_gather(cotangent, "mp", axis=1, tiled=True)
    cot_rows, mats_causal, mats_anti = lax.optimization_barrier((cot_rows, mats_causal, mats_anti))
    partial = exchange_contract(cot_rows, out_weight, ctx_count)
    grad_mixed = lax.psum_scatter(partial, "ctx", scatter_dimension=0, tiled=True)

    fwd = [(k, k + 1) for k in range(ctx_count - 1)]
    bwd = [(k + 1, k) for k in range(ctx_count - 1)]
    product = (key_act.astype(jnp.float32) * value_act.astype(jnp.float32)).astype(jnp.bfloat16)
    prev_tail = lax.ppermute(product[rows - halo :], "ctx", fwd)
    widened = jnp.concatenate([prev_tail, product], 0)
    win_prod = windows(widened, tiles, block, width)
    mixed = filter_apply(mats_causal, win_prod, local_groups, per_group)
    grad_mixed, mixed = lax.optimization_barrier((grad_mixed, mixed))

    grad_conv = (grad_mixed * query_act.astype(jnp.float32)).astype(jnp.bfloat16)
    next_head = lax.ppermute(grad_conv[:halo], "ctx", bwd)
    gc4 = grad_conv.reshape(tiles, block, local_groups, per_group)
    wp4 = win_prod.reshape(tiles, width, local_groups, per_group)
    cross = jnp.einsum("kigc,kjgc->gij", gc4, wp4, preferred_element_type=jnp.float32)
    i = lax.broadcasted_iota(jnp.int32, (block, width, flen), 0)
    j = lax.broadcasted_iota(jnp.int32, (block, width, flen), 1)
    lag = lax.broadcasted_iota(jnp.int32, (block, width, flen), 2) + zero
    pick = (i + halo - j == lag).astype(jnp.bfloat16)
    cross_hi = lax.reduce_precision(cross, exponent_bits=8, mantissa_bits=7)
    diag = None
    for piece in (cross_hi, cross - cross_hi):
        term = jnp.einsum("gij,ijs->gs", piece.astype(jnp.bfloat16), pick, preferred_element_type=jnp.float32)
        diag = term if diag is None else diag + term
    scale = (rows * ctx_count * per_group) ** (-0.5)
    diag, next_head = lax.optimization_barrier((diag, next_head))
    local_filters = butterfly_sum(diag, "ctx", ctx_count) * scale
    grad_filters = butterfly_gather(local_filters, "mp", mp_count)
    trailing = jnp.concatenate([grad_conv, next_head], 0)
    win_grad = windows(trailing, tiles, block, width)
    grad_product = filter_apply(mats_anti, win_grad, local_groups, per_group)
    grad_filters, grad_product = lax.optimization_barrier((grad_filters, grad_product))


    grad_query = (grad_mixed * mixed).astype(jnp.bfloat16)
    grad_key = (grad_product * value_act.astype(jnp.float32)).astype(jnp.bfloat16)
    grad_value = (grad_product * key_act.astype(jnp.float32)).astype(jnp.bfloat16)
    return (grad_query, grad_key, grad_value, grad_filters)


def solution(mesh):
    in_specs = (P("ctx", "mp"), P("mp", "ctx"), P("ctx", "mp"), P("ctx", "mp"), P("ctx", "mp"), P())
    out_specs = (P("ctx", "mp"), P("ctx", "mp"), P("ctx", "mp"), P())
    return jax.shard_map(body, mesh=mesh, in_specs=in_specs, out_specs=out_specs, check_vma=False)
```

```python
import jax
import jax.numpy as jnp
from jax import lax
from jax.sharding import PartitionSpec as P


def contract(left, right):
    return lax.dot_general(
        left, right, (((1,), (1,)), ((), ())), preferred_element_type=jnp.float32
    )


def toeplitz(seq, block, width):
    groups = seq.shape[0]
    flat = jnp.tile(seq, (1, block))[:, : block * width]
    return flat.reshape(groups, block, width)


def toeplitz_mats(taps, block, width, halo, causal, zero):
    groups, flen = taps.shape
    hi = lax.reduce_precision(taps, exponent_bits=8, mantissa_bits=7)
    both = jnp.concatenate([hi, taps - hi], 0).astype(jnp.bfloat16)
    i = lax.broadcasted_iota(jnp.int32, (block, width, flen), 0)
    j = lax.broadcasted_iota(jnp.int32, (block, width, flen), 1)
    s = lax.broadcasted_iota(jnp.int32, (block, width, flen), 2) + zero
    lag = i + halo - j if causal else j - i
    pick = (lag == s).astype(jnp.bfloat16)
    mats = jnp.einsum("gs,ijs->gij", both, pick, preferred_element_type=jnp.float32)
    mats = mats.astype(jnp.bfloat16)
    return mats[:groups], mats[groups:]


def split_bf16(x):
    hi = lax.reduce_precision(x, exponent_bits=8, mantissa_bits=7)
    lo = x - hi
    return hi.astype(jnp.bfloat16), lo.astype(jnp.bfloat16)


def windows(x, tiles, block, width):
    return jnp.stack([x[k * block : k * block + width] for k in range(tiles)])


def filter_apply(mat, wins, groups, per_group):
    tiles, width, chans = wins.shape
    w4 = wins.reshape(tiles, width, groups, per_group)
    both = jnp.einsum("gij,kjgc->kigc", mat, w4, preferred_element_type=jnp.float32)
    block = mat.shape[1] // 2
    return (both[:, :block] + both[:, block:]).reshape(tiles * block, chans)


def exchange_columns(x, count):
    rows, cols = x.shape
    width = cols // count
    me = lax.axis_index("ctx")
    out = jnp.zeros((count * rows, width), x.dtype)
    own = lax.dynamic_slice_in_dim(x, me * width, width, 1)
    out = lax.dynamic_update_slice_in_dim(out, own, me * rows, 0)
    for shift in range(1, count):
        dest = (me + shift) % count
        chunk = lax.dynamic_slice_in_dim(x, dest * width, width, 1)
        got = lax.ppermute(chunk, "ctx", [(k, (k + shift) % count) for k in range(count)])
        src = (me + count - shift) % count
        out = lax.dynamic_update_slice_in_dim(out, got, src * rows, 0)
    return out


def butterfly_sum(x, axis, count):
    if count & (count - 1):
        return lax.psum(x, axis)
    step = 1
    while step < count:
        x = x + lax.ppermute(x, axis, [(k, k ^ step) for k in range(count)])
        step *= 2
    return x


def butterfly_gather(x, axis, count):
    if count & (count - 1):
        return lax.all_gather(x, axis, axis=0, tiled=True)
    me = lax.axis_index(axis)
    step = 1
    while step < count:
        got = lax.ppermute(x, axis, [(k, k ^ step) for k in range(count)])
        low = (me // step) % 2 == 0
        x = jnp.where(low, jnp.concatenate([x, got]), jnp.concatenate([got, x]))
        step *= 2
    return x


def body(cotangent, out_weight, query_act, key_act, value_act, filters):
    rows, chans = cotangent.shape
    groups, flen = filters.shape
    ctx_count = lax.axis_size("ctx")
    mp_count = lax.axis_size("mp")
    per_group = chans * mp_count // groups
    local_groups = chans // per_group
    halo = flen
    block = 64 if rows % 64 == 0 else rows
    tiles = rows // block
    width = block + halo

    taps = lax.dynamic_slice_in_dim(filters, lax.axis_index("mp") * local_groups, local_groups, 0)
    pad = jnp.zeros((local_groups, width + 1 - flen - 1), jnp.float32)
    one = jnp.zeros((local_groups, 1), jnp.float32)
    seq_causal = jnp.concatenate([one, taps[:, ::-1], pad], 1)
    seq_anti = jnp.concatenate([taps, pad, one], 1)
    zero = lax.axis_index("ctx") // ctx_count
    mats_causal = toeplitz_mats(taps, block, width, halo, True, zero)
    mats_anti = toeplitz_mats(taps, block, width, halo, False, zero)

    cot_rows = lax.all_gather(cotangent, "mp", axis=1, tiled=True)
    mats_causal = jnp.concatenate(mats_causal, 1)
    mats_anti = jnp.concatenate(mats_anti, 1)
    cot_rows, mats_causal, mats_anti = lax.optimization_barrier((cot_rows, mats_causal, mats_anti))
    cot_cols = exchange_columns(cot_rows, ctx_count)
    partial = contract(cot_cols, out_weight)
    grad_mixed = lax.psum_scatter(partial, "ctx", scatter_dimension=0, tiled=True)

    fwd = [(k, k + 1) for k in range(ctx_count - 1)]
    bwd = [(k + 1, k) for k in range(ctx_count - 1)]
    product = (key_act.astype(jnp.float32) * value_act.astype(jnp.float32)).astype(jnp.bfloat16)
    prev_tail = lax.ppermute(product[rows - halo :], "ctx", fwd)
    widened = jnp.concatenate([prev_tail, product], 0)
    win_prod = windows(widened, tiles, block, width)
    mixed = filter_apply(mats_causal, win_prod, local_groups, per_group)
    grad_mixed, mixed = lax.optimization_barrier((grad_mixed, mixed))

    grad_conv = (grad_mixed * query_act.astype(jnp.float32)).astype(jnp.bfloat16)
    next_head = lax.ppermute(grad_conv[:halo], "ctx", bwd)
    gc4 = grad_conv.reshape(tiles, block, local_groups, per_group)
    wp4 = win_prod.reshape(tiles, width, local_groups, per_group)
    cross = jnp.einsum("kigc,kjgc->gij", gc4, wp4, preferred_element_type=jnp.float32)
    i = lax.broadcasted_iota(jnp.int32, (block, width, flen), 0)
    j = lax.broadcasted_iota(jnp.int32, (block, width, flen), 1)
    lag = lax.broadcasted_iota(jnp.int32, (block, width, flen), 2) + zero
    pick = (i + halo - j == lag).astype(jnp.bfloat16)
    cross_hi = lax.reduce_precision(cross, exponent_bits=8, mantissa_bits=7)
    diag = None
    for piece in (cross_hi, cross - cross_hi):
        term = jnp.einsum("gij,ijs->gs", piece.astype(jnp.bfloat16), pick, preferred_element_type=jnp.float32)
        diag = term if diag is None else diag + term
    scale = (rows * ctx_count * per_group) ** (-0.5)
    diag, next_head = lax.optimization_barrier((diag, next_head))
    local_filters = butterfly_sum(diag, "ctx", ctx_count) * scale
    grad_filters = butterfly_gather(local_filters, "mp", mp_count)
    trailing = jnp.concatenate([grad_conv, next_head], 0)
    win_grad = windows(trailing, tiles, block, width)
    grad_product = filter_apply(mats_anti, win_grad, local_groups, per_group)
    grad_filters, grad_product = lax.optimization_barrier((grad_filters, grad_product))


    grad_query = (grad_mixed * mixed).astype(jnp.bfloat16)
    grad_key = (grad_product * value_act.astype(jnp.float32)).astype(jnp.bfloat16)
    grad_value = (grad_product * key_act.astype(jnp.float32)).astype(jnp.bfloat16)
    return (grad_query, grad_key, grad_value, grad_filters)


def solution(mesh):
    in_specs = (P("ctx", "mp"), P("mp", "ctx"), P("ctx", "mp"), P("ctx", "mp"), P("ctx", "mp"), P())
    out_specs = (P("ctx", "mp"), P("ctx", "mp"), P("ctx", "mp"), P())
    return jax.shard_map(body, mesh=mesh, in_specs=in_specs, out_specs=out_specs, check_vma=False)
```

```python
import jax
import jax.numpy as jnp
from jax import lax
from jax.sharding import PartitionSpec as P


def contract(left, right):
    return lax.dot_general(
        left, right, (((1,), (1,)), ((), ())), preferred_element_type=jnp.float32
    )


def toeplitz(seq, block, width):
    groups = seq.shape[0]
    flat = jnp.tile(seq, (1, block))[:, : block * width]
    return flat.reshape(groups, block, width)


def toeplitz_mats(taps, block, width, halo, causal, zero):
    groups, flen = taps.shape
    hi = lax.reduce_precision(taps, exponent_bits=8, mantissa_bits=7)
    both = jnp.concatenate([hi, taps - hi], 0).astype(jnp.bfloat16)
    i = lax.broadcasted_iota(jnp.int32, (block, width, flen), 0)
    j = lax.broadcasted_iota(jnp.int32, (block, width, flen), 1)
    s = lax.broadcasted_iota(jnp.int32, (block, width, flen), 2) + zero
    lag = i + halo - j if causal else j - i
    pick = (lag == s).astype(jnp.bfloat16)
    mats = jnp.einsum("gs,ijs->gij", both, pick, preferred_element_type=jnp.float32)
    mats = mats.astype(jnp.bfloat16)
    return mats[:groups], mats[groups:]


def split_bf16(x):
    hi = lax.reduce_precision(x, exponent_bits=8, mantissa_bits=7)
    lo = x - hi
    return hi.astype(jnp.bfloat16), lo.astype(jnp.bfloat16)


def windows(x, tiles, block, width):
    return jnp.stack([x[k * block : k * block + width] for k in range(tiles)])


def filter_apply(mats, wins, groups, per_group):
    tiles, width, chans = wins.shape
    w4 = wins.reshape(tiles, width, groups, per_group)
    total = None
    for m in mats:
        part = jnp.einsum("gij,kjgc->kigc", m, w4, preferred_element_type=jnp.float32)
        total = part if total is None else total + part
    block = mats[0].shape[1]
    return total.reshape(tiles * block, chans)


def exchange_columns(x, count):
    rows, cols = x.shape
    width = cols // count
    me = lax.axis_index("ctx")
    out = jnp.zeros((count * rows, width), x.dtype)
    own = lax.dynamic_slice_in_dim(x, me * width, width, 1)
    out = lax.dynamic_update_slice_in_dim(out, own, me * rows, 0)
    for shift in range(1, count):
        dest = (me + shift) % count
        chunk = lax.dynamic_slice_in_dim(x, dest * width, width, 1)
        got = lax.ppermute(chunk, "ctx", [(k, (k + shift) % count) for k in range(count)])
        src = (me + count - shift) % count
        out = lax.dynamic_update_slice_in_dim(out, got, src * rows, 0)
    return out


def butterfly_sum(x, axis, count):
    if count & (count - 1):
        return lax.psum(x, axis)
    step = 1
    while step < count:
        x = x + lax.ppermute(x, axis, [(k, k ^ step) for k in range(count)])
        step *= 2
    return x


def butterfly_gather(x, axis, count):
    if count & (count - 1):
        return lax.all_gather(x, axis, axis=0, tiled=True)
    me = lax.axis_index(axis)
    step = 1
    while step < count:
        got = lax.ppermute(x, axis, [(k, k ^ step) for k in range(count)])
        low = (me // step) % 2 == 0
        x = jnp.where(low, jnp.concatenate([x, got]), jnp.concatenate([got, x]))
        step *= 2
    return x


def body(cotangent, out_weight, query_act, key_act, value_act, filters):
    rows, chans = cotangent.shape
    groups, flen = filters.shape
    ctx_count = lax.axis_size("ctx")
    mp_count = lax.axis_size("mp")
    per_group = chans * mp_count // groups
    local_groups = chans // per_group
    halo = flen
    block = 64 if rows % 64 == 0 else rows
    tiles = rows // block
    width = block + halo

    taps = lax.dynamic_slice_in_dim(filters, lax.axis_index("mp") * local_groups, local_groups, 0)
    pad = jnp.zeros((local_groups, width + 1 - flen - 1), jnp.float32)
    one = jnp.zeros((local_groups, 1), jnp.float32)
    seq_causal = jnp.concatenate([one, taps[:, ::-1], pad], 1)
    seq_anti = jnp.concatenate([taps, pad, one], 1)
    zero = lax.axis_index("ctx") // ctx_count
    mats_causal = toeplitz_mats(taps, block, width, halo, True, zero)
    mats_anti = toeplitz_mats(taps, block, width, halo, False, zero)

    cot_rows = lax.all_gather(cotangent, "mp", axis=1, tiled=True)
    cot_rows, mats_causal, mats_anti = lax.optimization_barrier((cot_rows, mats_causal, mats_anti))
    cot_cols = exchange_columns(cot_rows, ctx_count)
    partial = contract(cot_cols, out_weight)
    grad_mixed = lax.psum_scatter(partial, "ctx", scatter_dimension=0, tiled=True)

    fwd = [(k, k + 1) for k in range(ctx_count - 1)]
    bwd = [(k + 1, k) for k in range(ctx_count - 1)]
    product = (key_act.astype(jnp.float32) * value_act.astype(jnp.float32)).astype(jnp.bfloat16)
    prev_tail = lax.ppermute(product[rows - halo :], "ctx", fwd)
    widened = jnp.concatenate([prev_tail, product], 0)
    win_prod = windows(widened, tiles, block, width)
    mixed = filter_apply(mats_causal, win_prod, local_groups, per_group)
    grad_mixed, mixed = lax.optimization_barrier((grad_mixed, mixed))

    grad_conv = (grad_mixed * query_act.astype(jnp.float32)).astype(jnp.bfloat16)
    next_head = lax.ppermute(grad_conv[:halo], "ctx", bwd)
    gc4 = grad_conv.reshape(tiles, block, local_groups, per_group)
    wp4 = win_prod.reshape(tiles, width, local_groups, per_group)
    cross = jnp.einsum("kigc,kjgc->gij", gc4, wp4, preferred_element_type=jnp.float32)
    i = lax.broadcasted_iota(jnp.int32, (block, width, flen), 0)
    j = lax.broadcasted_iota(jnp.int32, (block, width, flen), 1)
    lag = lax.broadcasted_iota(jnp.int32, (block, width, flen), 2) + zero
    pick = (i + halo - j == lag).astype(jnp.bfloat16)
    cross_hi = lax.reduce_precision(cross, exponent_bits=8, mantissa_bits=7)
    diag = None
    for piece in (cross_hi, cross - cross_hi):
        term = jnp.einsum("gij,ijs->gs", piece.astype(jnp.bfloat16), pick, preferred_element_type=jnp.float32)
        diag = term if diag is None else diag + term
    scale = (rows * ctx_count * per_group) ** (-0.5)
    diag, next_head = lax.optimization_barrier((diag, next_head))
    local_filters = butterfly_sum(diag, "ctx", ctx_count) * scale
    grad_filters = butterfly_gather(local_filters, "mp", mp_count)
    trailing = jnp.concatenate([grad_conv, next_head], 0)
    win_grad = windows(trailing, tiles, block, width)
    grad_product = filter_apply(mats_anti, win_grad, local_groups, per_group)


    grad_query = (grad_mixed * mixed).astype(jnp.bfloat16)
    grad_key = (grad_product * value_act.astype(jnp.float32)).astype(jnp.bfloat16)
    grad_value = (grad_product * key_act.astype(jnp.float32)).astype(jnp.bfloat16)
    return (grad_query, grad_key, grad_value, grad_filters)


def solution(mesh):
    in_specs = (P("ctx", "mp"), P("mp", "ctx"), P("ctx", "mp"), P("ctx", "mp"), P("ctx", "mp"), P())
    out_specs = (P("ctx", "mp"), P("ctx", "mp"), P("ctx", "mp"), P())
    return jax.shard_map(body, mesh=mesh, in_specs=in_specs, out_specs=out_specs, check_vma=False)
```

```python
import jax
import jax.numpy as jnp
from jax import lax
from jax.sharding import PartitionSpec as P


def contract(left, right):
    return lax.dot_general(
        left, right, (((1,), (1,)), ((), ())), preferred_element_type=jnp.float32
    )


def toeplitz(seq, block, width):
    groups = seq.shape[0]
    flat = jnp.tile(seq, (1, block))[:, : block * width]
    return flat.reshape(groups, block, width)


def toeplitz_mats(taps, block, width, halo, causal, zero):
    groups, flen = taps.shape
    hi = lax.reduce_precision(taps, exponent_bits=8, mantissa_bits=7)
    both = jnp.concatenate([hi, taps - hi], 0).astype(jnp.bfloat16)
    i = lax.broadcasted_iota(jnp.int32, (block, width, flen), 0)
    j = lax.broadcasted_iota(jnp.int32, (block, width, flen), 1)
    s = lax.broadcasted_iota(jnp.int32, (block, width, flen), 2) + zero
    lag = i + halo - j if causal else j - i
    pick = (lag == s).astype(jnp.bfloat16)
    mats = jnp.einsum("gs,ijs->gij", both, pick, preferred_element_type=jnp.float32)
    mats = mats.astype(jnp.bfloat16)
    return mats[:groups], mats[groups:]


def split_bf16(x):
    hi = lax.reduce_precision(x, exponent_bits=8, mantissa_bits=7)
    lo = x - hi
    return hi.astype(jnp.bfloat16), lo.astype(jnp.bfloat16)


def windows(x, tiles, block, width):
    return jnp.stack([x[k * block : k * block + width] for k in range(tiles)])


def filter_apply(mats, wins, groups, per_group):
    tiles, width, chans = wins.shape
    w4 = wins.reshape(tiles, width, groups, per_group)
    total = None
    for m in mats:
        part = jnp.einsum("gij,kjgc->kigc", m, w4, preferred_element_type=jnp.float32)
        total = part if total is None else total + part
    block = mats[0].shape[1]
    return total.reshape(tiles * block, chans)


def exchange_columns(x, count):
    rows, cols = x.shape
    width = cols // count
    me = lax.axis_index("ctx")
    out = jnp.zeros((count * rows, width), x.dtype)
    own = lax.dynamic_slice_in_dim(x, me * width, width, 1)
    out = lax.dynamic_update_slice_in_dim(out, own, me * rows, 0)
    for shift in range(1, count):
        dest = (me + shift) % count
        chunk = lax.dynamic_slice_in_dim(x, dest * width, width, 1)
        got = lax.ppermute(chunk, "ctx", [(k, (k + shift) % count) for k in range(count)])
        src = (me + count - shift) % count
        out = lax.dynamic_update_slice_in_dim(out, got, src * rows, 0)
    return out


def butterfly_sum(x, axis, count):
    if count & (count - 1):
        return lax.psum(x, axis)
    step = 1
    while step < count:
        x = x + lax.ppermute(x, axis, [(k, k ^ step) for k in range(count)])
        step *= 2
    return x


def butterfly_gather(x, axis, count):
    if count & (count - 1):
        return lax.all_gather(x, axis, axis=0, tiled=True)
    me = lax.axis_index(axis)
    step = 1
    while step < count:
        got = lax.ppermute(x, axis, [(k, k ^ step) for k in range(count)])
        low = (me // step) % 2 == 0
        x = jnp.where(low, jnp.concatenate([x, got]), jnp.concatenate([got, x]))
        step *= 2
    return x


def body(cotangent, out_weight, query_act, key_act, value_act, filters):
    rows, chans = cotangent.shape
    groups, flen = filters.shape
    ctx_count = lax.axis_size("ctx")
    mp_count = lax.axis_size("mp")
    per_group = chans * mp_count // groups
    local_groups = chans // per_group
    halo = flen
    block = 64 if rows % 64 == 0 else rows
    tiles = rows // block
    width = block + halo

    taps = lax.dynamic_slice_in_dim(filters, lax.axis_index("mp") * local_groups, local_groups, 0)
    pad = jnp.zeros((local_groups, width + 1 - flen - 1), jnp.float32)
    one = jnp.zeros((local_groups, 1), jnp.float32)
    seq_causal = jnp.concatenate([one, taps[:, ::-1], pad], 1)
    seq_anti = jnp.concatenate([taps, pad, one], 1)
    zero = lax.axis_index("ctx") // ctx_count
    mats_causal = toeplitz_mats(taps, block, width, halo, True, zero)
    mats_anti = toeplitz_mats(taps, block, width, halo, False, zero)

    cot_rows = lax.all_gather(cotangent, "mp", axis=1, tiled=True)
    cot_rows, mats_causal, mats_anti = lax.optimization_barrier((cot_rows, mats_causal, mats_anti))
    cot_cols = exchange_columns(cot_rows, ctx_count)
    partial = contract(cot_cols, out_weight)
    grad_mixed = lax.psum_scatter(partial, "ctx", scatter_dimension=0, tiled=True)

    fwd = [(k, k + 1) for k in range(ctx_count - 1)]
    bwd = [(k + 1, k) for k in range(ctx_count - 1)]
    product = (key_act.astype(jnp.float32) * value_act.astype(jnp.float32)).astype(jnp.bfloat16)
    prev_tail = lax.ppermute(product[rows - halo :], "ctx", fwd)
    widened = jnp.concatenate([prev_tail, product], 0)
    win_prod = windows(widened, tiles, block, width)
    mixed = filter_apply(mats_causal, win_prod, local_groups, per_group)
    grad_mixed, mixed = lax.optimization_barrier((grad_mixed, mixed))

    grad_conv = (grad_mixed * query_act.astype(jnp.float32)).astype(jnp.bfloat16)
    next_head = lax.ppermute(grad_conv[:halo], "ctx", bwd)
    gc4 = grad_conv.reshape(tiles, block, local_groups, per_group)
    wp4 = win_prod.reshape(tiles, width, local_groups, per_group)
    cross = jnp.einsum("kigc,kjgc->gij", gc4, wp4, preferred_element_type=jnp.float32)
    i = lax.broadcasted_iota(jnp.int32, (block, width, flen), 0)
    j = lax.broadcasted_iota(jnp.int32, (block, width, flen), 1)
    lag = lax.broadcasted_iota(jnp.int32, (block, width, flen), 2) + zero
    pick = (i + halo - j == lag).astype(jnp.bfloat16)
    cross_hi = lax.reduce_precision(cross, exponent_bits=8, mantissa_bits=7)
    diag = None
    for piece in (cross_hi, cross - cross_hi):
        term = jnp.einsum("gij,ijs->gs", piece.astype(jnp.bfloat16), pick, preferred_element_type=jnp.float32)
        diag = term if diag is None else diag + term
    scale = (rows * ctx_count * per_group) ** (-0.5)
    local_filters = butterfly_sum(diag, "ctx", ctx_count) * scale
    grad_filters = butterfly_gather(local_filters, "mp", mp_count)
    trailing = jnp.concatenate([grad_conv, next_head], 0)
    win_grad = windows(trailing, tiles, block, width)
    grad_product = filter_apply(mats_anti, win_grad, local_groups, per_group)


    grad_query = (grad_mixed * mixed).astype(jnp.bfloat16)
    grad_key = (grad_product * value_act.astype(jnp.float32)).astype(jnp.bfloat16)
    grad_value = (grad_product * key_act.astype(jnp.float32)).astype(jnp.bfloat16)
    return (grad_query, grad_key, grad_value, grad_filters)


def solution(mesh):
    in_specs = (P("ctx", "mp"), P("mp", "ctx"), P("ctx", "mp"), P("ctx", "mp"), P("ctx", "mp"), P())
    out_specs = (P("ctx", "mp"), P("ctx", "mp"), P("ctx", "mp"), P())
    return jax.shard_map(body, mesh=mesh, in_specs=in_specs, out_specs=out_specs, check_vma=False)
```
